128 devices in a mesh: lat: 8 (over z, y_hi), lon: 16 (over x, y_lo, core).
Axes of the slice: x: 4, y: 4 (y_hi: 2, y_lo: 2; y = y_hi * 2 + y_lo), z: 4, core: 2. Of those that a mesh axis runs over, the one named last changes fastest.
Arguments:
- tracer: float32 [10, 768, 2048], P(None, 'lat', 'lon'), may hold values from -6 to 6
- velocity: float32 [10, 768, 2048], P(None, 'lat', 'lon'), may hold values from -6 to 6
- tracer_adjoint: float32 [10, 768, 2048], P(None, 'lat', 'lon'), may hold values from -6 to 6
- velocity_adjoint: float32 [10, 768, 2048], P(None, 'lat', 'lon'), may hold values from -6 to 6
- sea_mask: int32 [10, 768, 2048], P(None, 'lat', 'lon'), may hold values from 0 to 1, as said below
- face_east: float32 [768, 2048], P('lat', 'lon'), may hold values from 0.03 to 0.2
- face_north: float32 [768, 2048], P('lat', 'lon'), may hold values from 0.03 to 0.2
- viscosity: float32 [768, 2048], P('lat', 'lon'), may hold values from 0.1 to 0.7
- conv_first: float32 [3, 32, 20], replicated, may hold values from -0.75 to 0.75
- conv_middle: float32 [3, 32, 32], replicated, may hold values from -0.625 to 0.625
- conv_last: float32 [3, 20, 32], replicated, may hold values from -0.625 to 0.625
Outputs:
- tracer_grad: float32 [10, 768, 2048], P(None, 'lat', 'lon')
- velocity_grad: float32 [10, 768, 2048], P(None, 'lat', 'lon')
- first_grad: float32 [3, 32, 20], replicated
- middle_grad: float32 [3, 32, 32], replicated
- last_grad: float32 [3, 20, 32], replicated
The draws below stay inside these ranges and needn't reach their ends.
Inputs may be any that keep to these rules, and one draw needn't show every extreme that they name: `sea_mask`: in each column a cell is sea from the top level down to the column's depth and land below it; a depth may be zero (a land column).
All inputs are finite; a program needn't handle non-finite values.
Results may differ from the reference program's by a relative error of at most 0.00015.
Values sent between devices are 32-bit elements; how exact they have to be, the bound alone decides.
No kernel may reach another device: no remote copies, remote signals or barrier semaphores. Data moves between devices by JAX's collectives and lax.ppermute only.
A program may use at most 128 MiB of HBM per device.

```python
import math
import jax
import jax.numpy as jnp
from jax import lax

LEV = 10
CH = 32
KW = 3
CHIN = 20
NLAT = 768
NLON = 2048


def draw_sea_mask(key, part):
    depth = jax.random.randint(jax.random.fold_in(key, 11), (NLAT, NLON), 0, LEV + 1)
    levels = jnp.arange(LEV, dtype=jnp.int32)[:, None, None]
    return (levels < depth[None, :, :]).astype(jnp.int32)


def block_levels(stream_key, dims, split, low, top_value):
    def one(position, shards_of):
        draws = jax.random.uniform(jax.random.fold_in(jax.random.fold_in(stream_key, 6), position), (shards_of,), jnp.float32, low / len(split), top_value / len(split))
        return jnp.repeat(jnp.exp(draws), dims[position] // shards_of).reshape((-1,) + (1,) * (len(dims) - position - 1))

    level = one(*split[0])
    for cut in split[1:]:
        level = level * one(*cut)
    return level


def bell_draw(stream_key, extent, spread, limit, cuts=(), held_as=jnp.bfloat16):
    drawn = jax.random.normal(stream_key, extent, jnp.float32) * spread
    if len(cuts) > 0:
        drawn = block_levels(stream_key, extent, cuts, -0.22, 0.18) * drawn
    return jnp.clip(drawn, min=-limit, max=limit).astype(held_as)


def setup_inputs(seed: int = 0) -> dict:
    splits = jax.random.split(jax.random.key(seed), 12)
    tracer = bell_draw(splits[0], (LEV, NLAT, NLON), 1.0, 6.0, ((1, 8), (2, 16)), jnp.float32)
    velocity = bell_draw(splits[1], (LEV, NLAT, NLON), 1.0, 6.0, ((1, 8), (2, 16)), jnp.float32)
    tracer_adjoint = bell_draw(splits[2], (LEV, NLAT, NLON), 1.0, 6.0, ((1, 8), (2, 16)), jnp.float32)
    velocity_adjoint = bell_draw(splits[3], (LEV, NLAT, NLON), 1.0, 6.0, ((1, 8), (2, 16)), jnp.float32)
    sea_mask = draw_sea_mask(jax.random.fold_in(splits[11], 71), 0)
    face_east = jnp.clip(jnp.exp(math.log(0.2) - 1.89712 * jax.random.uniform(splits[5], (NLAT, NLON), jnp.float32) ** block_levels(splits[5], (NLAT, NLON), ((0, 8), (1, 16)), -0.2, 0.2)), 0.03, 0.2)
    face_north = jnp.clip(jnp.exp(math.log(0.2) - 1.89712 * jax.random.uniform(splits[6], (NLAT, NLON), jnp.float32) ** block_levels(splits[6], (NLAT, NLON), ((0, 8), (1, 16)), -0.2, 0.2)), 0.03, 0.2)
    viscosity = jnp.clip(jnp.exp(math.log(0.7) - 1.9459101 * jax.random.uniform(splits[7], (NLAT, NLON), jnp.float32) ** block_levels(splits[7], (NLAT, NLON), ((0, 8), (1, 16)), -0.2, 0.2)), 0.1, 0.7)
    conv_first = bell_draw(splits[8], (KW, CH, CHIN), (KW * CHIN) ** -0.5, 0.75, (), jnp.float32)
    conv_middle = bell_draw(splits[9], (KW, CH, CH), (KW * CH) ** -0.5, 0.625, (), jnp.float32)
    conv_last = bell_draw(splits[10], (KW, CHIN, CH), (KW * CH) ** -0.5, 0.625, (), jnp.float32)
    return dict(tracer=tracer, velocity=velocity, tracer_adjoint=tracer_adjoint, velocity_adjoint=velocity_adjoint, sea_mask=sea_mask, face_east=face_east, face_north=face_north, viscosity=viscosity, conv_first=conv_first, conv_middle=conv_middle, conv_last=conv_last)


highest = lax.Precision.HIGHEST

def pad_grid(values, margin):
    widths = [(0, 0)] * (values.ndim - 2) + [(margin, margin), (0, 0)]
    padded = jnp.pad(values, widths)
    return jnp.concatenate([padded[..., -margin:], padded, padded[..., :margin]], axis=-1)

def laplace(values, sea_pad, east_pad, north_pad):
    centre = values[..., 1:-1, 1:-1]
    sea_centre = sea_pad[..., 1:-1, 1:-1]
    summed = east_pad[1:-1, 1:-1] * sea_centre * sea_pad[..., 1:-1, 2:] * (values[..., 1:-1, 2:] - centre)
    summed = summed + east_pad[1:-1, :-2] * sea_pad[..., 1:-1, :-2] * sea_centre * (values[..., 1:-1, :-2] - centre)
    summed = summed + north_pad[1:-1, 1:-1] * sea_centre * sea_pad[..., 2:, 1:-1] * (values[..., 2:, 1:-1] - centre)
    summed = summed + north_pad[:-2, 1:-1] * sea_pad[..., :-2, 1:-1] * sea_centre * (values[..., :-2, 1:-1] - centre)
    return summed

def periodic_conv(kernel, values):
    summed = jnp.zeros((kernel.shape[1],) + values.shape[1:], jnp.float32)
    for offset in range(KW):
        shifted = jnp.roll(values, 1 - offset, axis=-1)
        summed = summed + jnp.einsum('oc,cyx->oyx', kernel[offset], shifted, precision=highest)
    return summed

def network(weights, values):
    hidden = jnp.tanh(periodic_conv(weights[0], values))
    hidden = jnp.tanh(periodic_conv(weights[1], hidden))
    return periodic_conv(weights[2], hidden)

def reference(tracer, velocity, tracer_adjoint, velocity_adjoint, sea_mask, face_east, face_north, viscosity, conv_first, conv_middle, conv_last):
    sea = sea_mask.astype(jnp.float32)
    sea_pad = pad_grid(sea, 1)
    east_pad = pad_grid(face_east, 1)
    north_pad = pad_grid(face_north, 1)

    def operator(values):
        return laplace(pad_grid(values, 1), sea_pad, east_pad, north_pad)

    def forward(tracer_in, velocity_in, weights):
        closure = network(weights, jnp.concatenate([tracer_in, velocity_in], axis=0))
        new_tracer = tracer_in + operator(tracer_in) + sea * closure[:LEV]
        new_velocity = velocity_in - operator(viscosity * operator(velocity_in)) + sea * closure[LEV:]
        return (new_tracer, new_velocity)
    weights = (conv_first, conv_middle, conv_last)
    outputs, pullback = jax.vjp(forward, tracer, velocity, weights)
    tracer_grad, velocity_grad, weight_grads = pullback((tracer_adjoint, velocity_adjoint))
    scale = 1.0 / math.sqrt(NLAT * NLON)
    return (tracer_grad, velocity_grad, weight_grads[0] * scale, weight_grads[1] * scale, weight_grads[2] * scale)
```

```python
import math

import jax
import jax.numpy as jnp
from jax import lax
from jax.sharding import PartitionSpec as P

KW = 3


highest = lax.Precision.HIGHEST


def with_halo(block, sides, width):
    for axis, dim in sides:
        count = lax.axis_size(axis)
        forward = [(i, i + 1) for i in range(count - 1)]
        forward.append((count - 1, 0))
        backward = [(target, source) for source, target in forward]
        low = lax.ppermute(
            lax.slice_in_dim(block, block.shape[dim] - width, None, axis=dim), axis, forward
        )
        high = lax.ppermute(lax.slice_in_dim(block, 0, width, axis=dim), axis, backward)
        block = jnp.concatenate([low, block, high], axis=dim)
    return block


def laplace(values, sea_pad, east_pad, north_pad):
    centre = values[..., 1:-1, 1:-1]
    sea_centre = sea_pad[..., 1:-1, 1:-1]
    summed = (
        east_pad[1:-1, 1:-1]
        * sea_centre
        * sea_pad[..., 1:-1, 2:]
        * (values[..., 1:-1, 2:] - centre)
    )
    summed = summed + east_pad[1:-1, :-2] * sea_pad[..., 1:-1, :-2] * sea_centre * (
        values[..., 1:-1, :-2] - centre
    )
    summed = summed + north_pad[1:-1, 1:-1] * sea_centre * sea_pad[..., 2:, 1:-1] * (
        values[..., 2:, 1:-1] - centre
    )
    summed = summed + north_pad[:-2, 1:-1] * sea_pad[..., :-2, 1:-1] * sea_centre * (
        values[..., :-2, 1:-1] - centre
    )
    return summed


def domain_rows(tile_rows, margin):
    start = lax.axis_index("lat") * tile_rows - margin
    global_row = start + jnp.arange(tile_rows + 2 * margin, dtype=jnp.int32)
    total_rows = tile_rows * lax.axis_size("lat")
    return ((global_row >= 0) & (global_row < total_rows)).astype(jnp.float32)[:, None]


def periodic_conv(kernel, values):
    summed = jnp.zeros((kernel.shape[1],) + values.shape[1:], jnp.float32)
    for offset in range(KW):
        shifted = jnp.roll(values, 1 - offset, axis=-1)
        summed = summed + jnp.einsum("oc,cyx->oyx", kernel[offset], shifted, precision=highest)
    return summed


def network(weights, values, convolve):
    hidden = jnp.tanh(convolve(weights[0], values))
    hidden = jnp.tanh(convolve(weights[1], hidden))
    return convolve(weights[2], hidden)


def periodic_network(weights, values):
    return network(weights, values, periodic_conv)


PACKED_ROWS = 128
LANES = 128


def pack(parts):
    flat = jnp.concatenate([part.reshape(-1) for part in parts])
    rows = max(PACKED_ROWS, -(-flat.shape[0] // LANES))
    flat = jnp.pad(flat, (0, rows * LANES - flat.shape[0]))
    return flat.reshape(rows, LANES)


def unpack(total, parts):
    total = total.reshape(-1)
    out, start = [], 0
    for part in parts:
        out.append(total[start : start + part.size].reshape(part.shape))
        start += part.size
    return out


def on_device(
    tracer,
    velocity,
    tracer_adjoint,
    velocity_adjoint,
    sea_mask,
    face_east,
    face_north,
    viscosity,
    conv_first,
    conv_middle,
    conv_last,
):
    levels = tracer.shape[0]
    tile_rows = tracer.shape[1]
    tile_cols = tracer.shape[2]
    sea_cells = sea_mask.astype(jnp.float32)
    planes = jnp.concatenate(
        [tracer_adjoint, velocity_adjoint, sea_cells, face_east[None], face_north[None]], axis=0
    )
    padded = with_halo(planes, (("lat", 1), ("lon", 2)), 1)
    weights = (conv_first, conv_middle, conv_last)
    inputs = jnp.concatenate([tracer, velocity], axis=0)
    masked_adjoint = jnp.concatenate(
        [tracer_adjoint * sea_cells, velocity_adjoint * sea_cells], axis=0
    )
    stacked = jnp.concatenate([inputs, masked_adjoint], axis=0)
    band = lax.all_to_all(stacked, "lon", split_axis=1, concat_axis=2, tiled=True)
    closure_out, pullback = jax.vjp(periodic_network, weights, band[: 2 * levels])
    weight_grads, band_grad = pullback(band[2 * levels :])
    packed = pack(weight_grads)
    packed, padded = lax.optimization_barrier((packed, padded))
    summed = unpack(lax.psum(packed, ("lat", "lon")), weight_grads)
    input_grad = lax.all_to_all(band_grad, "lon", split_axis=2, concat_axis=1, tiled=True)
    sea_pad = padded[2 * levels : 3 * levels] * domain_rows(tile_rows, 1)
    east_pad = padded[3 * levels]
    north_pad = padded[3 * levels + 1]
    tracer_term = laplace(padded[:levels], sea_pad, east_pad, north_pad)
    first_laplace = laplace(padded[levels : 2 * levels], sea_pad, east_pad, north_pad)
    scaled = viscosity * first_laplace
    scaled_pad = with_halo(scaled, (("lat", 1), ("lon", 2)), 1)
    viscous_term = laplace(scaled_pad, sea_pad, east_pad, north_pad)
    scale = 1.0 / math.sqrt(tile_rows * lax.axis_size("lat") * tile_cols * lax.axis_size("lon"))
    tracer_grad = tracer_adjoint + tracer_term + input_grad[:levels]
    velocity_grad = velocity_adjoint - viscous_term + input_grad[levels:]
    return (tracer_grad, velocity_grad, summed[0] * scale, summed[1] * scale, summed[2] * scale)


def solution(mesh):
    return jax.shard_map(
        on_device,
        mesh=mesh,
        in_specs=(
            P(None, "lat", "lon"),
            P(None, "lat", "lon"),
            P(None, "lat", "lon"),
            P(None, "lat", "lon"),
            P(None, "lat", "lon"),
            P("lat", "lon"),
            P("lat", "lon"),
            P("lat", "lon"),
            P(),
            P(),
            P(),
        ),
        out_specs=(P(None, "lat", "lon"), P(None, "lat", "lon"), P(), P(), P()),
        check_vma=False,
    )
```

```python
import math

import jax
import jax.numpy as jnp
from jax import lax
from jax.sharding import PartitionSpec as P

KW = 3


highest = lax.Precision.HIGHEST


def with_halo(block, sides, width):
    for axis, dim in sides:
        count = lax.axis_size(axis)
        forward = [(i, i + 1) for i in range(count - 1)]
        forward.append((count - 1, 0))
        backward = [(target, source) for source, target in forward]
        low = lax.ppermute(
            lax.slice_in_dim(block, block.shape[dim] - width, None, axis=dim), axis, forward
        )
        high = lax.ppermute(lax.slice_in_dim(block, 0, width, axis=dim), axis, backward)
        block = jnp.concatenate([low, block, high], axis=dim)
    return block


def laplace(values, sea_pad, east_pad, north_pad):
    centre = values[..., 1:-1, 1:-1]
    sea_centre = sea_pad[..., 1:-1, 1:-1]
    summed = (
        east_pad[1:-1, 1:-1]
        * sea_centre
        * sea_pad[..., 1:-1, 2:]
        * (values[..., 1:-1, 2:] - centre)
    )
    summed = summed + east_pad[1:-1, :-2] * sea_pad[..., 1:-1, :-2] * sea_centre * (
        values[..., 1:-1, :-2] - centre
    )
    summed = summed + north_pad[1:-1, 1:-1] * sea_centre * sea_pad[..., 2:, 1:-1] * (
        values[..., 2:, 1:-1] - centre
    )
    summed = summed + north_pad[:-2, 1:-1] * sea_pad[..., :-2, 1:-1] * sea_centre * (
        values[..., :-2, 1:-1] - centre
    )
    return summed


def domain_rows(tile_rows, margin):
    start = lax.axis_index("lat") * tile_rows - margin
    global_row = start + jnp.arange(tile_rows + 2 * margin, dtype=jnp.int32)
    total_rows = tile_rows * lax.axis_size("lat")
    return ((global_row >= 0) & (global_row < total_rows)).astype(jnp.float32)[:, None]


def periodic_conv(kernel, values):
    summed = jnp.zeros((kernel.shape[1],) + values.shape[1:], jnp.float32)
    for offset in range(KW):
        shifted = jnp.roll(values, 1 - offset, axis=-1)
        summed = summed + jnp.einsum("oc,cyx->oyx", kernel[offset], shifted, precision=highest)
    return summed


def network(weights, values, convolve):
    hidden = jnp.tanh(convolve(weights[0], values))
    hidden = jnp.tanh(convolve(weights[1], hidden))
    return convolve(weights[2], hidden)


def periodic_network(weights, values):
    return network(weights, values, periodic_conv)


LANES = 128


def butterfly_sum(values, axes):
    for axis in axes:
        size = lax.axis_size(axis)
        stride = 1
        while stride < size:
            pairs = [(i, i ^ stride) for i in range(size)]
            values = values + lax.ppermute(values, axis, pairs)
            stride *= 2
    return values


def pack(parts):
    flat = jnp.concatenate([part.reshape(-1) for part in parts])
    rows = -(-flat.shape[0] // LANES)
    flat = jnp.pad(flat, (0, rows * LANES - flat.shape[0]))
    return flat.reshape(rows, LANES)


def unpack(total, parts):
    total = total.reshape(-1)
    out, start = [], 0
    for part in parts:
        out.append(total[start : start + part.size].reshape(part.shape))
        start += part.size
    return out


def on_device(
    tracer,
    velocity,
    tracer_adjoint,
    velocity_adjoint,
    sea_mask,
    face_east,
    face_north,
    viscosity,
    conv_first,
    conv_middle,
    conv_last,
):
    levels = tracer.shape[0]
    tile_rows = tracer.shape[1]
    tile_cols = tracer.shape[2]
    sea_cells = sea_mask.astype(jnp.float32)
    planes = jnp.concatenate(
        [tracer_adjoint, velocity_adjoint, sea_cells, face_east[None], face_north[None]], axis=0
    )
    padded = with_halo(planes, (("lat", 1), ("lon", 2)), 1)
    weights = (conv_first, conv_middle, conv_last)
    inputs = jnp.concatenate([tracer, velocity], axis=0)
    masked_adjoint = jnp.concatenate(
        [tracer_adjoint * sea_cells, velocity_adjoint * sea_cells], axis=0
    )
    stacked = jnp.concatenate([inputs, masked_adjoint], axis=0)
    band = lax.all_to_all(stacked, "lon", split_axis=1, concat_axis=2, tiled=True)
    closure_out, pullback = jax.vjp(periodic_network, weights, band[: 2 * levels])
    weight_grads, band_grad = pullback(band[2 * levels :])
    packed = pack(weight_grads)
    packed, padded = lax.optimization_barrier((packed, padded))
    summed = unpack(butterfly_sum(packed, ("lon", "lat")), weight_grads)
    input_grad = lax.all_to_all(band_grad, "lon", split_axis=2, concat_axis=1, tiled=True)
    sea_pad = padded[2 * levels : 3 * levels] * domain_rows(tile_rows, 1)
    east_pad = padded[3 * levels]
    north_pad = padded[3 * levels + 1]
    tracer_term = laplace(padded[:levels], sea_pad, east_pad, north_pad)
    first_laplace = laplace(padded[levels : 2 * levels], sea_pad, east_pad, north_pad)
    scaled = viscosity * first_laplace
    scaled_pad = with_halo(scaled, (("lat", 1), ("lon", 2)), 1)
    viscous_term = laplace(scaled_pad, sea_pad, east_pad, north_pad)
    scale = 1.0 / math.sqrt(tile_rows * lax.axis_size("lat") * tile_cols * lax.axis_size("lon"))
    tracer_grad = tracer_adjoint + tracer_term + input_grad[:levels]
    velocity_grad = velocity_adjoint - viscous_term + input_grad[levels:]
    return (tracer_grad, velocity_grad, summed[0] * scale, summed[1] * scale, summed[2] * scale)


def solution(mesh):
    return jax.shard_map(
        on_device,
        mesh=mesh,
        in_specs=(
            P(None, "lat", "lon"),
            P(None, "lat", "lon"),
            P(None, "lat", "lon"),
            P(None, "lat", "lon"),
            P(None, "lat", "lon"),
            P("lat", "lon"),
            P("lat", "lon"),
            P("lat", "lon"),
            P(),
            P(),
            P(),
        ),
        out_specs=(P(None, "lat", "lon"), P(None, "lat", "lon"), P(), P(), P()),
        check_vma=False,
    )
```

```python
import math

import jax
import jax.numpy as jnp
from jax import lax
from jax.sharding import PartitionSpec as P

KW = 3


highest = lax.Precision.HIGH


def with_halo(block, sides, width):
    for axis, dim in sides:
        count = lax.axis_size(axis)
        forward = [(i, i + 1) for i in range(count - 1)]
        forward.append((count - 1, 0))
        backward = [(target, source) for source, target in forward]
        low = lax.ppermute(
            lax.slice_in_dim(block, block.shape[dim] - width, None, axis=dim), axis, forward
        )
        high = lax.ppermute(lax.slice_in_dim(block, 0, width, axis=dim), axis, backward)
        block = jnp.concatenate([low, block, high], axis=dim)
    return block


def laplace(values, sea_pad, east_pad, north_pad):
    centre = values[..., 1:-1, 1:-1]
    sea_centre = sea_pad[..., 1:-1, 1:-1]
    summed = (
        east_pad[1:-1, 1:-1]
        * sea_centre
        * sea_pad[..., 1:-1, 2:]
        * (values[..., 1:-1, 2:] - centre)
    )
    summed = summed + east_pad[1:-1, :-2] * sea_pad[..., 1:-1, :-2] * sea_centre * (
        values[..., 1:-1, :-2] - centre
    )
    summed = summed + north_pad[1:-1, 1:-1] * sea_centre * sea_pad[..., 2:, 1:-1] * (
        values[..., 2:, 1:-1] - centre
    )
    summed = summed + north_pad[:-2, 1:-1] * sea_pad[..., :-2, 1:-1] * sea_centre * (
        values[..., :-2, 1:-1] - centre
    )
    return summed


def domain_rows(tile_rows, margin):
    start = lax.axis_index("lat") * tile_rows - margin
    global_row = start + jnp.arange(tile_rows + 2 * margin, dtype=jnp.int32)
    total_rows = tile_rows * lax.axis_size("lat")
    return ((global_row >= 0) & (global_row < total_rows)).astype(jnp.float32)[:, None]


def periodic_conv(kernel, values):
    summed = jnp.zeros((kernel.shape[1],) + values.shape[1:], jnp.float32)
    for offset in range(KW):
        shifted = jnp.roll(values, 1 - offset, axis=-1)
        summed = summed + jnp.einsum("oc,cyx->oyx", kernel[offset], shifted, precision=highest)
    return summed


def network(weights, values, convolve):
    hidden = jnp.tanh(convolve(weights[0], values))
    hidden = jnp.tanh(convolve(weights[1], hidden))
    return convolve(weights[2], hidden)


def periodic_network(weights, values):
    return network(weights, values, periodic_conv)


LANES = 128


def butterfly_sum(values, axes):
    for axis in axes:
        size = lax.axis_size(axis)
        stride = 1
        while stride < size:
            pairs = [(i, i ^ stride) for i in range(size)]
            values = values + lax.ppermute(values, axis, pairs)
            stride *= 2
    return values


def pack(parts):
    flat = jnp.concatenate([part.reshape(-1) for part in parts])
    rows = -(-flat.shape[0] // LANES)
    flat = jnp.pad(flat, (0, rows * LANES - flat.shape[0]))
    return flat.reshape(rows, LANES)


def unpack(total, parts):
    total = total.reshape(-1)
    out, start = [], 0
    for part in parts:
        out.append(total[start : start + part.size].reshape(part.shape))
        start += part.size
    return out


def on_device(
    tracer,
    velocity,
    tracer_adjoint,
    velocity_adjoint,
    sea_mask,
    face_east,
    face_north,
    viscosity,
    conv_first,
    conv_middle,
    conv_last,
):
    levels = tracer.shape[0]
    tile_rows = tracer.shape[1]
    tile_cols = tracer.shape[2]
    sea_cells = sea_mask.astype(jnp.float32)
    planes = jnp.concatenate(
        [tracer_adjoint, velocity_adjoint, sea_cells, face_east[None], face_north[None]], axis=0
    )
    padded = with_halo(planes, (("lat", 1), ("lon", 2)), 1)
    weights = (conv_first, conv_middle, conv_last)
    inputs = jnp.concatenate([tracer, velocity], axis=0)
    masked_adjoint = jnp.concatenate(
        [tracer_adjoint * sea_cells, velocity_adjoint * sea_cells], axis=0
    )
    stacked = jnp.concatenate([inputs, masked_adjoint], axis=0)
    band = lax.all_to_all(stacked, "lon", split_axis=1, concat_axis=2, tiled=True)
    closure_out, pullback = jax.vjp(periodic_network, weights, band[: 2 * levels])
    weight_grads, band_grad = pullback(band[2 * levels :])
    packed = pack(weight_grads)
    packed, padded = lax.optimization_barrier((packed, padded))
    summed = unpack(butterfly_sum(packed, ("lon", "lat")), weight_grads)
    input_grad = lax.all_to_all(band_grad, "lon", split_axis=2, concat_axis=1, tiled=True)
    sea_pad = padded[2 * levels : 3 * levels] * domain_rows(tile_rows, 1)
    east_pad = padded[3 * levels]
    north_pad = padded[3 * levels + 1]
    tracer_term = laplace(padded[:levels], sea_pad, east_pad, north_pad)
    first_laplace = laplace(padded[levels : 2 * levels], sea_pad, east_pad, north_pad)
    scaled = viscosity * first_laplace
    scaled_pad = with_halo(scaled, (("lat", 1), ("lon", 2)), 1)
    viscous_term = laplace(scaled_pad, sea_pad, east_pad, north_pad)
    scale = 1.0 / math.sqrt(tile_rows * lax.axis_size("lat") * tile_cols * lax.axis_size("lon"))
    tracer_grad = tracer_adjoint + tracer_term + input_grad[:levels]
    velocity_grad = velocity_adjoint - viscous_term + input_grad[levels:]
    return (tracer_grad, velocity_grad, summed[0] * scale, summed[1] * scale, summed[2] * scale)


def solution(mesh):
    return jax.shard_map(
        on_device,
        mesh=mesh,
        in_specs=(
            P(None, "lat", "lon"),
            P(None, "lat", "lon"),
            P(None, "lat", "lon"),
            P(None, "lat", "lon"),
            P(None, "lat", "lon"),
            P("lat", "lon"),
            P("lat", "lon"),
            P("lat", "lon"),
            P(),
            P(),
            P(),
        ),
        out_specs=(P(None, "lat", "lon"), P(None, "lat", "lon"), P(), P(), P()),
        check_vma=False,
    )
```

```python
import math

import jax
import jax.numpy as jnp
from jax import lax
from jax.sharding import PartitionSpec as P

KW = 3


highest = lax.Precision.HIGH


def edges(block):
    def ring(axis, step):
        count = lax.axis_size(axis)
        return [(i, (i + step) % count) for i in range(count)]

    below = lax.ppermute(block[..., -1:, :], "lat", ring("lat", 1))
    above = lax.ppermute(block[..., :1, :], "lat", ring("lat", -1))
    left = lax.ppermute(block[..., :, -1:], "lon", ring("lon", 1))
    right = lax.ppermute(block[..., :, :1], "lon", ring("lon", -1))
    return below, above, left, right


def shifted(block, halo):
    below, above, left, right = halo
    east = jnp.concatenate([block[..., :, 1:], right], axis=-1)
    west = jnp.concatenate([left, block[..., :, :-1]], axis=-1)
    north = jnp.concatenate([block[..., 1:, :], above], axis=-2)
    south = jnp.concatenate([below, block[..., :-1, :]], axis=-2)
    return east, west, north, south


def laplace(values, value_halo, sea, sea_near, face_east, face_west, face_north, face_south):
    east, west, north, south = shifted(values, value_halo)
    sea_east, sea_west, sea_north, sea_south = sea_near
    summed = face_east * sea * sea_east * (east - values)
    summed = summed + face_west * sea_west * sea * (west - values)
    summed = summed + face_north * sea * sea_north * (north - values)
    summed = summed + face_south * sea_south * sea * (south - values)
    return summed


def row_inside(step):
    index = lax.axis_index("lat") + step
    return ((index >= 0) & (index < lax.axis_size("lat"))).astype(jnp.float32)


def lon_roll(values, step):
    if step == 1:
        return jnp.concatenate([jnp.roll(values[..., -1:], 1, axis=0), values[..., :-1]], axis=-1)
    if step == -1:
        return jnp.concatenate([values[..., 1:], jnp.roll(values[..., :1], -1, axis=0)], axis=-1)
    return values


def periodic_conv(kernel, values):
    summed = None
    for offset in range(KW):
        shifted = lon_roll(values, 1 - offset)
        term = jnp.einsum("oc,scml->soml", kernel[offset], shifted, precision=highest)
        summed = term if summed is None else summed + term
    return summed


def network(weights, values, convolve):
    hidden = jnp.tanh(convolve(weights[0], values))
    hidden = jnp.tanh(convolve(weights[1], hidden))
    return convolve(weights[2], hidden)


def periodic_network(weights, values):
    return network(weights, values, periodic_conv)


LANES = 128


def butterfly_sum(values, axes):
    for axis in axes:
        size = lax.axis_size(axis)
        stride = 1
        while stride < size:
            pairs = [(i, i ^ stride) for i in range(size)]
            values = values + lax.ppermute(values, axis, pairs)
            stride *= 2
    return values


def pack(parts):
    flat = jnp.concatenate([part.reshape(-1) for part in parts])
    rows = -(-flat.shape[0] // LANES)
    flat = jnp.pad(flat, (0, rows * LANES - flat.shape[0]))
    return flat.reshape(rows, LANES)


def unpack(total, parts):
    total = total.reshape(-1)
    out, start = [], 0
    for part in parts:
        out.append(total[start : start + part.size].reshape(part.shape))
        start += part.size
    return out


def on_device(
    tracer,
    velocity,
    tracer_adjoint,
    velocity_adjoint,
    sea_mask,
    face_east,
    face_north,
    viscosity,
    conv_first,
    conv_middle,
    conv_last,
):
    levels = tracer.shape[0]
    tile_rows = tracer.shape[1]
    tile_cols = tracer.shape[2]
    sea_cells = sea_mask.astype(jnp.float32)
    planes = jnp.concatenate(
        [tracer_adjoint, velocity_adjoint, sea_cells, face_east[None], face_north[None]], axis=0
    )
    plane_halo = edges(planes)
    weights = (conv_first, conv_middle, conv_last)
    inputs = jnp.concatenate([tracer, velocity], axis=0)
    masked_adjoint = jnp.concatenate(
        [tracer_adjoint * sea_cells, velocity_adjoint * sea_cells], axis=0
    )
    stacked = jnp.concatenate([inputs, masked_adjoint], axis=0)
    blocks = lax.axis_size("lon")
    chunks = stacked.reshape(stacked.shape[0], tile_rows // blocks, blocks, tile_cols)
    band = lax.all_to_all(chunks.transpose(2, 0, 1, 3), "lon", split_axis=0, concat_axis=0, tiled=True)
    closure_out, pullback = jax.vjp(periodic_network, weights, band[:, : 2 * levels])
    weight_grads, band_grad = pullback(band[:, 2 * levels :])
    packed = pack(weight_grads)
    packed, plane_halo = lax.optimization_barrier((packed, plane_halo))
    summed = unpack(butterfly_sum(packed, ("lon", "lat")), weight_grads)
    returned = lax.all_to_all(band_grad, "lon", split_axis=0, concat_axis=0, tiled=True)
    input_grad = returned.transpose(1, 2, 0, 3).reshape(2 * levels, tile_rows, tile_cols)
    below, above, left, right = plane_halo
    below = below * row_inside(-1)
    above = above * row_inside(1)

    def part(lo, hi):
        return tuple(piece[lo:hi] for piece in (below, above, left, right))

    sea_near = shifted(sea_cells, part(2 * levels, 3 * levels))
    face_west = jnp.concatenate([left[3 * levels], face_east[:, :-1]], axis=-1)
    face_south = jnp.concatenate([below[3 * levels + 1], face_north[:-1, :]], axis=-2)
    faces = (face_east, face_west, face_north, face_south)
    tracer_term = laplace(tracer_adjoint, part(0, levels), sea_cells, sea_near, *faces)
    first_laplace = laplace(velocity_adjoint, part(levels, 2 * levels), sea_cells, sea_near, *faces)
    scaled = viscosity * first_laplace
    viscous_term = laplace(scaled, edges(scaled), sea_cells, sea_near, *faces)
    scale = 1.0 / math.sqrt(tile_rows * lax.axis_size("lat") * tile_cols * lax.axis_size("lon"))
    tracer_grad = tracer_adjoint + tracer_term + input_grad[:levels]
    velocity_grad = velocity_adjoint - viscous_term + input_grad[levels:]
    return (tracer_grad, velocity_grad, summed[0] * scale, summed[1] * scale, summed[2] * scale)


def solution(mesh):
    return jax.shard_map(
        on_device,
        mesh=mesh,
        in_specs=(
            P(None, "lat", "lon"),
            P(None, "lat", "lon"),
            P(None, "lat", "lon"),
            P(None, "lat", "lon"),
            P(None, "lat", "lon"),
            P("lat", "lon"),
            P("lat", "lon"),
            P("lat", "lon"),
            P(),
            P(),
            P(),
        ),
        out_specs=(P(None, "lat", "lon"), P(None, "lat", "lon"), P(), P(), P()),
        check_vma=False,
    )
```

```python
import math

import jax
import jax.numpy as jnp
from jax import lax
from jax.sharding import PartitionSpec as P

KW = 3


highest = lax.Precision.HIGH


def edges(block):
    def ring(axis, step):
        count = lax.axis_size(axis)
        return [(i, (i + step) % count) for i in range(count)]

    below = lax.ppermute(block[..., -1:, :], "lat", ring("lat", 1))
    above = lax.ppermute(block[..., :1, :], "lat", ring("lat", -1))
    left = lax.ppermute(block[..., :, -1:], "lon", ring("lon", 1))
    right = lax.ppermute(block[..., :, :1], "lon", ring("lon", -1))
    return below, above, left, right


def shifted(block, halo):
    below, above, left, right = halo
    east = jnp.concatenate([block[..., :, 1:], right], axis=-1)
    west = jnp.concatenate([left, block[..., :, :-1]], axis=-1)
    north = jnp.concatenate([block[..., 1:, :], above], axis=-2)
    south = jnp.concatenate([below, block[..., :-1, :]], axis=-2)
    return east, west, north, south


def laplace(values, value_halo, sea, sea_near, face_east, face_west, face_north, face_south):
    east, west, north, south = shifted(values, value_halo)
    sea_east, sea_west, sea_north, sea_south = sea_near
    summed = face_east * sea * sea_east * (east - values)
    summed = summed + face_west * sea_west * sea * (west - values)
    summed = summed + face_north * sea * sea_north * (north - values)
    summed = summed + face_south * sea_south * sea * (south - values)
    return summed


def row_inside(step):
    index = lax.axis_index("lat") + step
    return ((index >= 0) & (index < lax.axis_size("lat"))).astype(jnp.float32)


def lon_roll(values, step):
    if step == 1:
        return jnp.concatenate([jnp.roll(values[..., -1:], 1, axis=0), values[..., :-1]], axis=-1)
    if step == -1:
        return jnp.concatenate([values[..., 1:], jnp.roll(values[..., :1], -1, axis=0)], axis=-1)
    return values


def stack_taps(values):
    return jnp.concatenate([lon_roll(values, 1), values, lon_roll(values, -1)], axis=1)


def unstack_taps(stacked, channels):
    first = lon_roll(stacked[:, :channels], -1)
    middle = stacked[:, channels : 2 * channels]
    last = lon_roll(stacked[:, 2 * channels :], 1)
    return first + middle + last


def flat_kernel(kernel):
    taps, outs, ins = kernel.shape
    return kernel.transpose(1, 0, 2).reshape(outs, taps * ins)


def kernel_of(flat, taps):
    outs, width = flat.shape
    return flat.reshape(outs, taps, width // taps).transpose(1, 0, 2)


def apply(flat, stacked):
    return jnp.einsum("oc,scml->soml", flat, stacked, precision=highest)


def network_vjp(weights, values, adjoint):
    flats = [flat_kernel(weight) for weight in weights]
    taps = weights[0].shape[0]
    in_stack = stack_taps(values)
    first = jnp.tanh(apply(flats[0], in_stack))
    first_stack = stack_taps(first)
    second = jnp.tanh(apply(flats[1], first_stack))
    second_stack = stack_taps(second)
    last_grad = jnp.einsum("soml,scml->oc", adjoint, second_stack, precision=highest)
    back = jnp.einsum("oc,soml->scml", flats[2], adjoint, precision=highest)
    second_delta = unstack_taps(back, second.shape[1]) * (1.0 - second * second)
    middle_grad = jnp.einsum("soml,scml->oc", second_delta, first_stack, precision=highest)
    back = jnp.einsum("oc,soml->scml", flats[1], second_delta, precision=highest)
    first_delta = unstack_taps(back, first.shape[1]) * (1.0 - first * first)
    first_grad = jnp.einsum("soml,scml->oc", first_delta, in_stack, precision=highest)
    back = jnp.einsum("oc,soml->scml", flats[0], first_delta, precision=highest)
    input_grad = unstack_taps(back, values.shape[1])
    grads = (kernel_of(first_grad, taps), kernel_of(middle_grad, taps), kernel_of(last_grad, taps))
    return grads, input_grad


LANES = 128


def butterfly_sum(values, axes):
    for axis in axes:
        size = lax.axis_size(axis)
        stride = 1
        while stride < size:
            pairs = [(i, i ^ stride) for i in range(size)]
            values = values + lax.ppermute(values, axis, pairs)
            stride *= 2
    return values


def pack(parts):
    flat = jnp.concatenate([part.reshape(-1) for part in parts])
    rows = -(-flat.shape[0] // LANES)
    flat = jnp.pad(flat, (0, rows * LANES - flat.shape[0]))
    return flat.reshape(rows, LANES)


def unpack(total, parts):
    total = total.reshape(-1)
    out, start = [], 0
    for part in parts:
        out.append(total[start : start + part.size].reshape(part.shape))
        start += part.size
    return out


def on_device(
    tracer,
    velocity,
    tracer_adjoint,
    velocity_adjoint,
    sea_mask,
    face_east,
    face_north,
    viscosity,
    conv_first,
    conv_middle,
    conv_last,
):
    levels = tracer.shape[0]
    tile_rows = tracer.shape[1]
    tile_cols = tracer.shape[2]
    sea_cells = sea_mask.astype(jnp.float32)
    planes = jnp.concatenate(
        [tracer_adjoint, velocity_adjoint, sea_cells, face_east[None], face_north[None]], axis=0
    )
    plane_halo = edges(planes)
    weights = (conv_first, conv_middle, conv_last)
    inputs = jnp.concatenate([tracer, velocity], axis=0)
    masked_adjoint = jnp.concatenate(
        [tracer_adjoint * sea_cells, velocity_adjoint * sea_cells], axis=0
    )
    stacked = jnp.concatenate([inputs, masked_adjoint], axis=0)
    blocks = lax.axis_size("lon")
    chunks = stacked.reshape(stacked.shape[0], tile_rows // blocks, blocks, tile_cols)
    band = lax.all_to_all(chunks.transpose(2, 0, 1, 3), "lon", split_axis=0, concat_axis=0, tiled=True)
    weight_grads, band_grad = network_vjp(weights, band[:, : 2 * levels], band[:, 2 * levels :])
    packed = pack(weight_grads)
    packed, plane_halo = lax.optimization_barrier((packed, plane_halo))
    summed = unpack(butterfly_sum(packed, ("lon", "lat")), weight_grads)
    returned = lax.all_to_all(band_grad, "lon", split_axis=0, concat_axis=0, tiled=True)
    input_grad = returned.transpose(1, 2, 0, 3).reshape(2 * levels, tile_rows, tile_cols)
    below, above, left, right = plane_halo
    below = below * row_inside(-1)
    above = above * row_inside(1)

    def part(lo, hi):
        return tuple(piece[lo:hi] for piece in (below, above, left, right))

    sea_near = shifted(sea_cells, part(2 * levels, 3 * levels))
    face_west = jnp.concatenate([left[3 * levels], face_east[:, :-1]], axis=-1)
    face_south = jnp.concatenate([below[3 * levels + 1], face_north[:-1, :]], axis=-2)
    faces = (face_east, face_west, face_north, face_south)
    tracer_term = laplace(tracer_adjoint, part(0, levels), sea_cells, sea_near, *faces)
    first_laplace = laplace(velocity_adjoint, part(levels, 2 * levels), sea_cells, sea_near, *faces)
    scaled = viscosity * first_laplace
    viscous_term = laplace(scaled, edges(scaled), sea_cells, sea_near, *faces)
    scale = 1.0 / math.sqrt(tile_rows * lax.axis_size("lat") * tile_cols * lax.axis_size("lon"))
    tracer_grad = tracer_adjoint + tracer_term + input_grad[:levels]
    velocity_grad = velocity_adjoint - viscous_term + input_grad[levels:]
    return (tracer_grad, velocity_grad, summed[0] * scale, summed[1] * scale, summed[2] * scale)


def solution(mesh):
    return jax.shard_map(
        on_device,
        mesh=mesh,
        in_specs=(
            P(None, "lat", "lon"),
            P(None, "lat", "lon"),
            P(None, "lat", "lon"),
            P(None, "lat", "lon"),
            P(None, "lat", "lon"),
            P("lat", "lon"),
            P("lat", "lon"),
            P("lat", "lon"),
            P(),
            P(),
            P(),
        ),
        out_specs=(P(None, "lat", "lon"), P(None, "lat", "lon"), P(), P(), P()),
        check_vma=False,
    )
```

```python
import math

import jax
import jax.numpy as jnp
from jax import lax
from jax.sharding import PartitionSpec as P

KW = 3


highest = lax.Precision.HIGH


def edges(block):
    def ring(axis, step):
        count = lax.axis_size(axis)
        return [(i, (i + step) % count) for i in range(count)]

    below = lax.ppermute(block[..., -1:, :], "lat", ring("lat", 1))
    above = lax.ppermute(block[..., :1, :], "lat", ring("lat", -1))
    left = lax.ppermute(block[..., :, -1], "lon", ring("lon", 1))
    right = lax.ppermute(block[..., :, 0], "lon", ring("lon", -1))
    return below, above, left, right


def shifted(block, halo):
    below, above, left, right = halo
    east = jnp.concatenate([block[..., :, 1:], right[..., None]], axis=-1)
    west = jnp.concatenate([left[..., None], block[..., :, :-1]], axis=-1)
    north = jnp.concatenate([block[..., 1:, :], above], axis=-2)
    south = jnp.concatenate([below, block[..., :-1, :]], axis=-2)
    return east, west, north, south


def laplace(values, value_halo, sea, sea_near, face_east, face_west, face_north, face_south):
    east, west, north, south = shifted(values, value_halo)
    sea_east, sea_west, sea_north, sea_south = sea_near
    summed = face_east * sea * sea_east * (east - values)
    summed = summed + face_west * sea_west * sea * (west - values)
    summed = summed + face_north * sea * sea_north * (north - values)
    summed = summed + face_south * sea_south * sea * (south - values)
    return summed


def row_inside(step):
    index = lax.axis_index("lat") + step
    return ((index >= 0) & (index < lax.axis_size("lat"))).astype(jnp.float32)


def lon_roll(values, step):
    if step == 1:
        return jnp.concatenate([jnp.roll(values[..., -1:], 1, axis=0), values[..., :-1]], axis=-1)
    if step == -1:
        return jnp.concatenate([values[..., 1:], jnp.roll(values[..., :1], -1, axis=0)], axis=-1)
    return values


def stack_taps(values):
    return jnp.concatenate([lon_roll(values, 1), values, lon_roll(values, -1)], axis=1)


def unstack_taps(stacked, channels):
    first = lon_roll(stacked[:, :channels], -1)
    middle = stacked[:, channels : 2 * channels]
    last = lon_roll(stacked[:, 2 * channels :], 1)
    return first + middle + last


def flat_kernel(kernel):
    return jnp.concatenate([kernel[tap] for tap in range(kernel.shape[0])], axis=1)


def kernel_of(flat, taps):
    width = flat.shape[1] // taps
    return jnp.stack([flat[:, tap * width : (tap + 1) * width] for tap in range(taps)])


def apply(flat, stacked):
    return jnp.einsum("oc,scml->soml", flat, stacked, precision=highest)


def network_vjp(weights, values, adjoint):
    flats = [flat_kernel(weight) for weight in weights]
    taps = weights[0].shape[0]
    in_stack = stack_taps(values)
    first = jnp.tanh(apply(flats[0], in_stack))
    first_stack = stack_taps(first)
    second = jnp.tanh(apply(flats[1], first_stack))
    second_stack = stack_taps(second)
    last_grad = jnp.einsum("soml,scml->oc", adjoint, second_stack, precision=highest)
    back = jnp.einsum("oc,soml->scml", flats[2], adjoint, precision=highest)
    second_delta = unstack_taps(back, second.shape[1]) * (1.0 - second * second)
    middle_grad = jnp.einsum("soml,scml->oc", second_delta, first_stack, precision=highest)
    back = jnp.einsum("oc,soml->scml", flats[1], second_delta, precision=highest)
    first_delta = unstack_taps(back, first.shape[1]) * (1.0 - first * first)
    first_grad = jnp.einsum("soml,scml->oc", first_delta, in_stack, precision=highest)
    back = jnp.einsum("oc,soml->scml", flats[0], first_delta, precision=highest)
    input_grad = unstack_taps(back, values.shape[1])
    grads = (kernel_of(first_grad, taps), kernel_of(middle_grad, taps), kernel_of(last_grad, taps))
    return grads, input_grad


LANES = 128


def butterfly_sum(values, axes):
    for axis in axes:
        size = lax.axis_size(axis)
        stride = 1
        while stride < size:
            pairs = [(i, i ^ stride) for i in range(size)]
            values = values + lax.ppermute(values, axis, pairs)
            stride *= 2
    return values


def pack(parts):
    flat = jnp.concatenate([part.reshape(-1) for part in parts])
    rows = -(-flat.shape[0] // LANES)
    flat = jnp.pad(flat, (0, rows * LANES - flat.shape[0]))
    return flat.reshape(rows, LANES)


def unpack(total, parts):
    total = total.reshape(-1)
    out, start = [], 0
    for part in parts:
        out.append(total[start : start + part.size].reshape(part.shape))
        start += part.size
    return out


def on_device(
    tracer,
    velocity,
    tracer_adjoint,
    velocity_adjoint,
    sea_mask,
    face_east,
    face_north,
    viscosity,
    conv_first,
    conv_middle,
    conv_last,
):
    levels = tracer.shape[0]
    tile_rows = tracer.shape[1]
    tile_cols = tracer.shape[2]
    sea_cells = sea_mask.astype(jnp.float32)
    planes = jnp.concatenate(
        [tracer_adjoint, velocity_adjoint, sea_cells, face_east[None], face_north[None]], axis=0
    )
    plane_halo = edges(planes)
    weights = (conv_first, conv_middle, conv_last)
    inputs = jnp.concatenate([tracer, velocity], axis=0)
    masked_adjoint = jnp.concatenate(
        [tracer_adjoint * sea_cells, velocity_adjoint * sea_cells], axis=0
    )
    stacked = jnp.concatenate([inputs, masked_adjoint], axis=0)
    blocks = lax.axis_size("lon")
    chunks = stacked.reshape(stacked.shape[0], tile_rows // blocks, blocks, tile_cols)
    band = lax.all_to_all(chunks.transpose(2, 0, 1, 3), "lon", split_axis=0, concat_axis=0, tiled=True)
    weight_grads, band_grad = network_vjp(weights, band[:, : 2 * levels], band[:, 2 * levels :])
    packed = pack(weight_grads)
    packed, plane_halo = lax.optimization_barrier((packed, plane_halo))
    summed = unpack(butterfly_sum(packed, ("lon", "lat")), weight_grads)
    returned = lax.all_to_all(band_grad, "lon", split_axis=0, concat_axis=0, tiled=True)
    input_grad = returned.transpose(1, 2, 0, 3).reshape(2 * levels, tile_rows, tile_cols)
    below, above, left, right = plane_halo
    below = below * row_inside(-1)
    above = above * row_inside(1)

    def part(lo, hi):
        return tuple(piece[lo:hi] for piece in (below, above, left, right))

    sea_near = shifted(sea_cells, part(2 * levels, 3 * levels))
    face_west = jnp.concatenate([left[3 * levels][:, None], face_east[:, :-1]], axis=-1)
    face_south = jnp.concatenate([below[3 * levels + 1], face_north[:-1, :]], axis=-2)
    faces = (face_east, face_west, face_north, face_south)
    tracer_term = laplace(tracer_adjoint, part(0, levels), sea_cells, sea_near, *faces)
    first_laplace = laplace(velocity_adjoint, part(levels, 2 * levels), sea_cells, sea_near, *faces)
    scaled = viscosity * first_laplace
    viscous_term = laplace(scaled, edges(scaled), sea_cells, sea_near, *faces)
    scale = 1.0 / math.sqrt(tile_rows * lax.axis_size("lat") * tile_cols * lax.axis_size("lon"))
    tracer_grad = tracer_adjoint + tracer_term + input_grad[:levels]
    velocity_grad = velocity_adjoint - viscous_term + input_grad[levels:]
    return (tracer_grad, velocity_grad, summed[0] * scale, summed[1] * scale, summed[2] * scale)


def solution(mesh):
    return jax.shard_map(
        on_device,
        mesh=mesh,
        in_specs=(
            P(None, "lat", "lon"),
            P(None, "lat", "lon"),
            P(None, "lat", "lon"),
            P(None, "lat", "lon"),
            P(None, "lat", "lon"),
            P("lat", "lon"),
            P("lat", "lon"),
            P("lat", "lon"),
            P(),
            P(),
            P(),
        ),
        out_specs=(P(None, "lat", "lon"), P(None, "lat", "lon"), P(), P(), P()),
        check_vma=False,
    )
```

```python
import math

import jax
import jax.numpy as jnp
from jax import lax
from jax.sharding import PartitionSpec as P

KW = 3


highest = lax.Precision.HIGH


def edges(block):
    def ring(axis, step):
        count = lax.axis_size(axis)
        return [(i, (i + step) % count) for i in range(count)]

    below = lax.ppermute(block[..., -1:, :], "lat", ring("lat", 1))
    above = lax.ppermute(block[..., :1, :], "lat", ring("lat", -1))
    left = lax.ppermute(block[..., :, -1:], "lon", ring("lon", 1))
    right = lax.ppermute(block[..., :, :1], "lon", ring("lon", -1))
    return below, above, left, right


def shifted(block, halo):
    below, above, left, right = halo
    east = jnp.concatenate([block[..., :, 1:], right], axis=-1)
    west = jnp.concatenate([left, block[..., :, :-1]], axis=-1)
    north = jnp.concatenate([block[..., 1:, :], above], axis=-2)
    south = jnp.concatenate([below, block[..., :-1, :]], axis=-2)
    return east, west, north, south


def laplace(values, value_halo, sea, sea_near, face_east, face_west, face_north, face_south):
    east, west, north, south = shifted(values, value_halo)
    sea_east, sea_west, sea_north, sea_south = sea_near
    summed = face_east * sea * sea_east * (east - values)
    summed = summed + face_west * sea_west * sea * (west - values)
    summed = summed + face_north * sea * sea_north * (north - values)
    summed = summed + face_south * sea_south * sea * (south - values)
    return summed


def row_inside(step):
    index = lax.axis_index("lat") + step
    return ((index >= 0) & (index < lax.axis_size("lat"))).astype(jnp.float32)


def lon_roll(values, step):
    if step == 1:
        return jnp.concatenate([jnp.roll(values[..., -1:], 1, axis=0), values[..., :-1]], axis=-1)
    if step == -1:
        return jnp.concatenate([values[..., 1:], jnp.roll(values[..., :1], -1, axis=0)], axis=-1)
    return values


def stack_taps(values):
    return jnp.concatenate([lon_roll(values, 1), values, lon_roll(values, -1)], axis=1)


def unstack_taps(stacked, channels):
    first = lon_roll(stacked[:, :channels], -1)
    middle = stacked[:, channels : 2 * channels]
    last = lon_roll(stacked[:, 2 * channels :], 1)
    return first + middle + last


def flat_kernel(kernel):
    return jnp.concatenate([kernel[tap] for tap in range(kernel.shape[0])], axis=1)


def kernel_of(flat, taps):
    width = flat.shape[1] // taps
    return jnp.stack([flat[:, tap * width : (tap + 1) * width] for tap in range(taps)])


def apply(flat, stacked):
    return jnp.einsum("oc,scml->soml", flat, stacked, precision=highest)


def network_vjp(weights, values, adjoint):
    flats = [flat_kernel(weight) for weight in weights]
    taps = weights[0].shape[0]
    in_stack = stack_taps(values)
    first = jnp.tanh(apply(flats[0], in_stack))
    first_stack = stack_taps(first)
    second = jnp.tanh(apply(flats[1], first_stack))
    second_stack = stack_taps(second)
    last_grad = jnp.einsum("soml,scml->oc", adjoint, second_stack, precision=highest)
    back = jnp.einsum("oc,soml->scml", flats[2], adjoint, precision=highest)
    second_delta = unstack_taps(back, second.shape[1]) * (1.0 - second * second)
    middle_grad = jnp.einsum("soml,scml->oc", second_delta, first_stack, precision=highest)
    back = jnp.einsum("oc,soml->scml", flats[1], second_delta, precision=highest)
    first_delta = unstack_taps(back, first.shape[1]) * (1.0 - first * first)
    first_grad = jnp.einsum("soml,scml->oc", first_delta, in_stack, precision=highest)
    back = jnp.einsum("oc,soml->scml", flats[0], first_delta, precision=highest)
    input_grad = unstack_taps(back, values.shape[1])
    grads = (kernel_of(first_grad, taps), kernel_of(middle_grad, taps), kernel_of(last_grad, taps))
    return grads, input_grad


LANES = 128


def butterfly_sum(values, axes):
    for axis in axes:
        size = lax.axis_size(axis)
        stride = 1
        while stride < size:
            pairs = [(i, i ^ stride) for i in range(size)]
            values = values + lax.ppermute(values, axis, pairs)
            stride *= 2
    return values


def pack(parts):
    flat = jnp.concatenate([part.reshape(-1) for part in parts])
    rows = -(-flat.shape[0] // LANES)
    flat = jnp.pad(flat, (0, rows * LANES - flat.shape[0]))
    return flat.reshape(rows, LANES)


def unpack(total, parts):
    total = total.reshape(-1)
    out, start = [], 0
    for part in parts:
        out.append(total[start : start + part.size].reshape(part.shape))
        start += part.size
    return out


def on_device(
    tracer,
    velocity,
    tracer_adjoint,
    velocity_adjoint,
    sea_mask,
    face_east,
    face_north,
    viscosity,
    conv_first,
    conv_middle,
    conv_last,
):
    levels = tracer.shape[0]
    tile_rows = tracer.shape[1]
    tile_cols = tracer.shape[2]
    sea_cells = sea_mask.astype(jnp.float32)
    planes = jnp.concatenate(
        [tracer_adjoint, velocity_adjoint, sea_cells, face_east[None], face_north[None]], axis=0
    )
    plane_halo = edges(planes)
    weights = (conv_first, conv_middle, conv_last)
    inputs = jnp.concatenate([tracer, velocity], axis=0)
    masked_adjoint = jnp.concatenate(
        [tracer_adjoint * sea_cells, velocity_adjoint * sea_cells], axis=0
    )
    stacked = jnp.concatenate([inputs, masked_adjoint], axis=0)
    blocks = lax.axis_size("lon")
    chunks = stacked.reshape(stacked.shape[0], tile_rows // blocks, blocks, tile_cols)
    band = lax.all_to_all(chunks.transpose(2, 0, 1, 3), "lon", split_axis=0, concat_axis=0, tiled=True)
    weight_grads, band_grad = network_vjp(weights, band[:, : 2 * levels], band[:, 2 * levels :])
    packed = pack(weight_grads)
    packed, plane_halo = lax.optimization_barrier((packed, plane_halo))
    summed = unpack(butterfly_sum(packed, ("lon", "lat")), weight_grads)
    returned = lax.all_to_all(band_grad, "lon", split_axis=0, concat_axis=0, tiled=True)
    input_grad = returned.transpose(1, 2, 0, 3).reshape(2 * levels, tile_rows, tile_cols)
    below, above, left, right = plane_halo
    below = below * row_inside(-1)
    above = above * row_inside(1)

    def part(lo, hi):
        return tuple(piece[lo:hi] for piece in (below, above, left, right))

    sea_near = shifted(sea_cells, part(2 * levels, 3 * levels))
    face_west = jnp.concatenate([left[3 * levels], face_east[:, :-1]], axis=-1)
    face_south = jnp.concatenate([below[3 * levels + 1], face_north[:-1, :]], axis=-2)
    faces = (face_east, face_west, face_north, face_south)
    tracer_term = laplace(tracer_adjoint, part(0, levels), sea_cells, sea_near, *faces)
    first_laplace = laplace(velocity_adjoint, part(levels, 2 * levels), sea_cells, sea_near, *faces)
    scaled = viscosity * first_laplace
    viscous_term = laplace(scaled, edges(scaled), sea_cells, sea_near, *faces)
    scale = 1.0 / math.sqrt(tile_rows * lax.axis_size("lat") * tile_cols * lax.axis_size("lon"))
    tracer_grad = tracer_adjoint + tracer_term + input_grad[:levels]
    velocity_grad = velocity_adjoint - viscous_term + input_grad[levels:]
    return (tracer_grad, velocity_grad, summed[0] * scale, summed[1] * scale, summed[2] * scale)


def solution(mesh):
    return jax.shard_map(
        on_device,
        mesh=mesh,
        in_specs=(
            P(None, "lat", "lon"),
            P(None, "lat", "lon"),
            P(None, "lat", "lon"),
            P(None, "lat", "lon"),
            P(None, "lat", "lon"),
            P("lat", "lon"),
            P("lat", "lon"),
            P("lat", "lon"),
            P(),
            P(),
            P(),
        ),
        out_specs=(P(None, "lat", "lon"), P(None, "lat", "lon"), P(), P(), P()),
        check_vma=False,
    )
```

```python
import math

import jax
import jax.numpy as jnp
from jax import lax
from jax.sharding import PartitionSpec as P

KW = 3


highest = lax.Precision.HIGH


def edges(block):
    def ring(axis, step):
        count = lax.axis_size(axis)
        return [(i, (i + step) % count) for i in range(count)]

    below = lax.ppermute(block[..., -1:, :], "lat", ring("lat", 1))
    above = lax.ppermute(block[..., :1, :], "lat", ring("lat", -1))
    left = lax.ppermute(block[..., :, -1:], "lon", ring("lon", 1))
    right = lax.ppermute(block[..., :, :1], "lon", ring("lon", -1))
    return below, above, left, right


def shifted(block, halo):
    below, above, left, right = halo
    east = jnp.concatenate([block[..., :, 1:], right], axis=-1)
    west = jnp.concatenate([left, block[..., :, :-1]], axis=-1)
    north = jnp.concatenate([block[..., 1:, :], above], axis=-2)
    south = jnp.concatenate([below, block[..., :-1, :]], axis=-2)
    return east, west, north, south


def laplace(values, value_halo, sea, sea_near, face_east, face_west, face_north, face_south):
    east, west, north, south = shifted(values, value_halo)
    sea_east, sea_west, sea_north, sea_south = sea_near
    summed = face_east * sea * sea_east * (east - values)
    summed = summed + face_west * sea_west * sea * (west - values)
    summed = summed + face_north * sea * sea_north * (north - values)
    summed = summed + face_south * sea_south * sea * (south - values)
    return summed


def row_inside(step):
    index = lax.axis_index("lat") + step
    return ((index >= 0) & (index < lax.axis_size("lat"))).astype(jnp.float32)


def lon_roll(values, step):
    if step == 1:
        return jnp.concatenate([jnp.roll(values[..., -1:], 1, axis=0), values[..., :-1]], axis=-1)
    if step == -1:
        return jnp.concatenate([values[..., 1:], jnp.roll(values[..., :1], -1, axis=0)], axis=-1)
    return values


def stack_taps(values):
    return jnp.concatenate([lon_roll(values, 1), values, lon_roll(values, -1)], axis=1)


def unstack_taps(stacked, channels):
    first = lon_roll(stacked[:, :channels], -1)
    middle = stacked[:, channels : 2 * channels]
    last = lon_roll(stacked[:, 2 * channels :], 1)
    return first + middle + last


def flat_kernel(kernel):
    taps, outs, ins = kernel.shape
    return kernel.transpose(1, 0, 2).reshape(outs, taps * ins)


def kernel_of(flat, taps):
    outs, width = flat.shape
    return flat.reshape(outs, taps, width // taps).transpose(1, 0, 2)


def apply(flat, stacked):
    return jnp.einsum("oc,scml->soml", flat, stacked, precision=highest)


def network_vjp(weights, values, adjoint):
    flats = [flat_kernel(weight) for weight in weights]
    taps = weights[0].shape[0]
    in_stack = stack_taps(values)
    first = jnp.tanh(apply(flats[0], in_stack))
    first_stack = stack_taps(first)
    second = jnp.tanh(apply(flats[1], first_stack))
    second_stack = stack_taps(second)
    last_grad = jnp.einsum("soml,scml->oc", adjoint, second_stack, precision=highest)
    back = jnp.einsum("oc,soml->scml", flats[2], adjoint, precision=highest)
    second_delta = unstack_taps(back, second.shape[1]) * (1.0 - second * second)
    middle_grad = jnp.einsum("soml,scml->oc", second_delta, first_stack, precision=highest)
    back = jnp.einsum("oc,soml->scml", flats[1], second_delta, precision=highest)
    first_delta = unstack_taps(back, first.shape[1]) * (1.0 - first * first)
    first_grad = jnp.einsum("soml,scml->oc", first_delta, in_stack, precision=highest)
    back = jnp.einsum("oc,soml->scml", flats[0], first_delta, precision=highest)
    input_grad = unstack_taps(back, values.shape[1])
    grads = (kernel_of(first_grad, taps), kernel_of(middle_grad, taps), kernel_of(last_grad, taps))
    return grads, input_grad


LANES = 128


def butterfly_sum(values, axes, tie=None):
    for index, axis in enumerate(axes):
        if index == 1 and tie is not None:
            values, tie = lax.optimization_barrier((values, tie))
        size = lax.axis_size(axis)
        stride = 1
        while stride < size:
            pairs = [(i, i ^ stride) for i in range(size)]
            values = values + lax.ppermute(values, axis, pairs)
            stride *= 2
    return values, tie


def pack(parts):
    flat = jnp.concatenate([part.reshape(-1) for part in parts])
    rows = -(-flat.shape[0] // LANES)
    flat = jnp.pad(flat, (0, rows * LANES - flat.shape[0]))
    return flat.reshape(rows, LANES)


def unpack(total, parts):
    total = total.reshape(-1)
    out, start = [], 0
    for part in parts:
        out.append(total[start : start + part.size].reshape(part.shape))
        start += part.size
    return out


def on_device(
    tracer,
    velocity,
    tracer_adjoint,
    velocity_adjoint,
    sea_mask,
    face_east,
    face_north,
    viscosity,
    conv_first,
    conv_middle,
    conv_last,
):
    levels = tracer.shape[0]
    tile_rows = tracer.shape[1]
    tile_cols = tracer.shape[2]
    sea_cells = sea_mask.astype(jnp.float32)
    planes = jnp.concatenate(
        [tracer_adjoint, velocity_adjoint, sea_cells, face_east[None], face_north[None]], axis=0
    )
    plane_halo = edges(planes)
    weights = (conv_first, conv_middle, conv_last)
    inputs = jnp.concatenate([tracer, velocity], axis=0)
    masked_adjoint = jnp.concatenate(
        [tracer_adjoint * sea_cells, velocity_adjoint * sea_cells], axis=0
    )
    stacked = jnp.concatenate([inputs, masked_adjoint], axis=0)
    blocks = lax.axis_size("lon")
    chunks = stacked.reshape(stacked.shape[0], tile_rows // blocks, blocks, tile_cols)
    band = lax.all_to_all(chunks.transpose(2, 0, 1, 3), "lon", split_axis=0, concat_axis=0, tiled=True)
    weight_grads, band_grad = network_vjp(weights, band[:, : 2 * levels], band[:, 2 * levels :])
    packed = pack(weight_grads)
    packed, plane_halo = lax.optimization_barrier((packed, plane_halo))
    returned = lax.all_to_all(band_grad, "lon", split_axis=0, concat_axis=0, tiled=True)
    input_grad = returned.transpose(1, 2, 0, 3).reshape(2 * levels, tile_rows, tile_cols)
    below, above, left, right = plane_halo
    below = below * row_inside(-1)
    above = above * row_inside(1)

    def part(lo, hi):
        return tuple(piece[lo:hi] for piece in (below, above, left, right))

    sea_near = shifted(sea_cells, part(2 * levels, 3 * levels))
    face_west = jnp.concatenate([left[3 * levels], face_east[:, :-1]], axis=-1)
    face_south = jnp.concatenate([below[3 * levels + 1], face_north[:-1, :]], axis=-2)
    faces = (face_east, face_west, face_north, face_south)
    tracer_term = laplace(tracer_adjoint, part(0, levels), sea_cells, sea_near, *faces)
    first_laplace = laplace(velocity_adjoint, part(levels, 2 * levels), sea_cells, sea_near, *faces)
    scaled = viscosity * first_laplace
    total, scaled_halo = butterfly_sum(packed, ("lon", "lat"), edges(scaled))
    summed = unpack(total, weight_grads)
    viscous_term = laplace(scaled, scaled_halo, sea_cells, sea_near, *faces)
    scale = 1.0 / math.sqrt(tile_rows * lax.axis_size("lat") * tile_cols * lax.axis_size("lon"))
    tracer_grad = tracer_adjoint + tracer_term + input_grad[:levels]
    velocity_grad = velocity_adjoint - viscous_term + input_grad[levels:]
    return (tracer_grad, velocity_grad, summed[0] * scale, summed[1] * scale, summed[2] * scale)


def solution(mesh):
    return jax.shard_map(
        on_device,
        mesh=mesh,
        in_specs=(
            P(None, "lat", "lon"),
            P(None, "lat", "lon"),
            P(None, "lat", "lon"),
            P(None, "lat", "lon"),
            P(None, "lat", "lon"),
            P("lat", "lon"),
            P("lat", "lon"),
            P("lat", "lon"),
            P(),
            P(),
            P(),
        ),
        out_specs=(P(None, "lat", "lon"), P(None, "lat", "lon"), P(), P(), P()),
        check_vma=False,
    )
```

```python
import math

import jax
import jax.numpy as jnp
from jax import lax
from jax.sharding import PartitionSpec as P

KW = 3


highest = lax.Precision.HIGH


def edges(block):
    def ring(axis, step):
        count = lax.axis_size(axis)
        return [(i, (i + step) % count) for i in range(count)]

    below = lax.ppermute(block[..., -1:, :], "lat", ring("lat", 1))
    above = lax.ppermute(block[..., :1, :], "lat", ring("lat", -1))
    left = lax.ppermute(block[..., :, -1:], "lon", ring("lon", 1))
    right = lax.ppermute(block[..., :, :1], "lon", ring("lon", -1))
    return below, above, left, right


def shifted(block, halo):
    below, above, left, right = halo
    east = jnp.concatenate([block[..., :, 1:], right], axis=-1)
    west = jnp.concatenate([left, block[..., :, :-1]], axis=-1)
    north = jnp.concatenate([block[..., 1:, :], above], axis=-2)
    south = jnp.concatenate([below, block[..., :-1, :]], axis=-2)
    return east, west, north, south


def laplace(values, value_halo, sea, sea_near, face_east, face_west, face_north, face_south):
    east, west, north, south = shifted(values, value_halo)
    sea_east, sea_west, sea_north, sea_south = sea_near
    summed = face_east * sea * sea_east * (east - values)
    summed = summed + face_west * sea_west * sea * (west - values)
    summed = summed + face_north * sea * sea_north * (north - values)
    summed = summed + face_south * sea_south * sea * (south - values)
    return summed


def row_inside(step):
    index = lax.axis_index("lat") + step
    return ((index >= 0) & (index < lax.axis_size("lat"))).astype(jnp.float32)


def lon_roll(values, step):
    if step == 1:
        return jnp.concatenate([jnp.roll(values[..., -1:], 1, axis=0), values[..., :-1]], axis=-1)
    if step == -1:
        return jnp.concatenate([values[..., 1:], jnp.roll(values[..., :1], -1, axis=0)], axis=-1)
    return values


def stack_taps(values):
    return jnp.concatenate([lon_roll(values, 1), values, lon_roll(values, -1)], axis=1)


def unstack_taps(stacked, channels):
    first = lon_roll(stacked[:, :channels], -1)
    middle = stacked[:, channels : 2 * channels]
    last = lon_roll(stacked[:, 2 * channels :], 1)
    return first + middle + last


def flat_kernel(kernel):
    taps, outs, ins = kernel.shape
    return kernel.transpose(1, 0, 2).reshape(outs, taps * ins)


def kernel_of(flat, taps):
    outs, width = flat.shape
    return flat.reshape(outs, taps, width // taps).transpose(1, 0, 2)


def apply(flat, stacked):
    return jnp.einsum("oc,scml->soml", flat, stacked, precision=highest)


def network_vjp(weights, values, adjoint):
    flats = [flat_kernel(weight) for weight in weights]
    taps = weights[0].shape[0]
    in_stack = stack_taps(values)
    first = jnp.tanh(apply(flats[0], in_stack))
    first_stack = stack_taps(first)
    second = jnp.tanh(apply(flats[1], first_stack))
    second_stack = stack_taps(second)
    last_grad = jnp.einsum("soml,scml->oc", adjoint, second_stack, precision=highest)
    back = jnp.einsum("oc,soml->scml", flats[2], adjoint, precision=highest)
    second_delta = unstack_taps(back, second.shape[1]) * (1.0 - second * second)
    middle_grad = jnp.einsum("soml,scml->oc", second_delta, first_stack, precision=highest)
    back = jnp.einsum("oc,soml->scml", flats[1], second_delta, precision=highest)
    first_delta = unstack_taps(back, first.shape[1]) * (1.0 - first * first)
    first_grad = jnp.einsum("soml,scml->oc", first_delta, in_stack, precision=highest)
    back = jnp.einsum("oc,soml->scml", flats[0], first_delta, precision=highest)
    input_grad = unstack_taps(back, values.shape[1])
    grads = (kernel_of(first_grad, taps), kernel_of(middle_grad, taps), kernel_of(last_grad, taps))
    return grads, input_grad


LANES = 128


def butterfly_sum(values, axes):
    for axis in axes:
        size = lax.axis_size(axis)
        stride = 1
        while stride < size:
            pairs = [(i, i ^ stride) for i in range(size)]
            values = values + lax.ppermute(values, axis, pairs)
            stride *= 2
    return values


def pack(parts):
    flat = jnp.concatenate([part.reshape(-1) for part in parts])
    rows = -(-flat.shape[0] // LANES)
    flat = jnp.pad(flat, (0, rows * LANES - flat.shape[0]))
    return flat.reshape(rows, LANES)


def unpack(total, parts):
    total = total.reshape(-1)
    out, start = [], 0
    for part in parts:
        out.append(total[start : start + part.size].reshape(part.shape))
        start += part.size
    return out


def on_device(
    tracer,
    velocity,
    tracer_adjoint,
    velocity_adjoint,
    sea_mask,
    face_east,
    face_north,
    viscosity,
    conv_first,
    conv_middle,
    conv_last,
):
    levels = tracer.shape[0]
    tile_rows = tracer.shape[1]
    tile_cols = tracer.shape[2]
    sea_cells = sea_mask.astype(jnp.float32)
    planes = jnp.concatenate(
        [tracer_adjoint, velocity_adjoint, sea_cells, face_east[None], face_north[None]], axis=0
    )
    plane_halo = edges(planes)
    weights = (conv_first, conv_middle, conv_last)
    inputs = jnp.concatenate([tracer, velocity], axis=0)
    masked_adjoint = jnp.concatenate(
        [tracer_adjoint * sea_cells, velocity_adjoint * sea_cells], axis=0
    )
    stacked = jnp.concatenate([inputs, masked_adjoint], axis=0)
    blocks = lax.axis_size("lon")
    chunks = stacked.reshape(stacked.shape[0], tile_rows // blocks, blocks, tile_cols)
    band = lax.all_to_all(chunks.transpose(2, 0, 1, 3), "lon", split_axis=0, concat_axis=0, tiled=True)
    weight_grads, band_grad = network_vjp(weights, band[:, : 2 * levels], band[:, 2 * levels :])
    scale = 1.0 / math.sqrt(tile_rows * lax.axis_size("lat") * tile_cols * lax.axis_size("lon"))
    packed = pack(weight_grads) * scale
    packed, plane_halo = lax.optimization_barrier((packed, plane_halo))
    summed = unpack(butterfly_sum(packed, ("lon", "lat")), weight_grads)
    returned = lax.all_to_all(band_grad, "lon", split_axis=0, concat_axis=0, tiled=True)
    input_grad = returned.transpose(1, 2, 0, 3).reshape(2 * levels, tile_rows, tile_cols)
    below, above, left, right = plane_halo
    below = below * row_inside(-1)
    above = above * row_inside(1)

    def part(lo, hi):
        return tuple(piece[lo:hi] for piece in (below, above, left, right))

    sea_near = shifted(sea_cells, part(2 * levels, 3 * levels))
    face_west = jnp.concatenate([left[3 * levels], face_east[:, :-1]], axis=-1)
    face_south = jnp.concatenate([below[3 * levels + 1], face_north[:-1, :]], axis=-2)
    faces = (face_east, face_west, face_north, face_south)
    tracer_term = laplace(tracer_adjoint, part(0, levels), sea_cells, sea_near, *faces)
    first_laplace = laplace(velocity_adjoint, part(levels, 2 * levels), sea_cells, sea_near, *faces)
    scaled = viscosity * first_laplace
    viscous_term = laplace(scaled, edges(scaled), sea_cells, sea_near, *faces)
    tracer_grad = tracer_adjoint + tracer_term + input_grad[:levels]
    velocity_grad = velocity_adjoint - viscous_term + input_grad[levels:]
    return (tracer_grad, velocity_grad, summed[0], summed[1], summed[2])


def solution(mesh):
    return jax.shard_map(
        on_device,
        mesh=mesh,
        in_specs=(
            P(None, "lat", "lon"),
            P(None, "lat", "lon"),
            P(None, "lat", "lon"),
            P(None, "lat", "lon"),
            P(None, "lat", "lon"),
            P("lat", "lon"),
            P("lat", "lon"),
            P("lat", "lon"),
            P(),
            P(),
            P(),
        ),
        out_specs=(P(None, "lat", "lon"), P(None, "lat", "lon"), P(), P(), P()),
        check_vma=False,
    )
```

```python
import math

import jax
import jax.numpy as jnp
from jax import lax
from jax.sharding import PartitionSpec as P

KW = 3


highest = lax.Precision.HIGH


def edges(block):
    def ring(axis, step):
        count = lax.axis_size(axis)
        return [(i, (i + step) % count) for i in range(count)]

    below = lax.ppermute(block[..., -1:, :], "lat", ring("lat", 1))
    above = lax.ppermute(block[..., :1, :], "lat", ring("lat", -1))
    left = lax.ppermute(block[..., :, -1:], "lon", ring("lon", 1))
    right = lax.ppermute(block[..., :, :1], "lon", ring("lon", -1))
    return below, above, left, right


def shifted(block, halo):
    below, above, left, right = halo
    east = jnp.concatenate([block[..., :, 1:], right], axis=-1)
    west = jnp.concatenate([left, block[..., :, :-1]], axis=-1)
    north = jnp.concatenate([block[..., 1:, :], above], axis=-2)
    south = jnp.concatenate([below, block[..., :-1, :]], axis=-2)
    return east, west, north, south


def laplace(values, value_halo, sea, sea_near, face_east, face_west, face_north, face_south):
    east, west, north, south = shifted(values, value_halo)
    sea_east, sea_west, sea_north, sea_south = sea_near
    summed = face_east * sea * sea_east * (east - values)
    summed = summed + face_west * sea_west * sea * (west - values)
    summed = summed + face_north * sea * sea_north * (north - values)
    summed = summed + face_south * sea_south * sea * (south - values)
    return summed


def row_inside(step):
    index = lax.axis_index("lat") + step
    return ((index >= 0) & (index < lax.axis_size("lat"))).astype(jnp.float32)


def lon_roll(values, step):
    if step == 1:
        return jnp.concatenate([jnp.roll(values[..., -1:], 1, axis=0), values[..., :-1]], axis=-1)
    if step == -1:
        return jnp.concatenate([values[..., 1:], jnp.roll(values[..., :1], -1, axis=0)], axis=-1)
    return values


def stack_taps(values):
    return jnp.concatenate([lon_roll(values, 1), values, lon_roll(values, -1)], axis=1)


def unstack_taps(stacked, channels):
    first = lon_roll(stacked[:, :channels], -1)
    middle = stacked[:, channels : 2 * channels]
    last = lon_roll(stacked[:, 2 * channels :], 1)
    return first + middle + last


def flat_kernel(kernel):
    taps, outs, ins = kernel.shape
    return kernel.transpose(1, 0, 2).reshape(outs, taps * ins)


def kernel_of(flat, taps):
    outs, width = flat.shape
    return flat.reshape(outs, taps, width // taps).transpose(1, 0, 2)


def apply(flat, stacked):
    return jnp.einsum("oc,scml->soml", flat, stacked, precision=highest)


def network_vjp(weights, values, adjoint):
    flats = [flat_kernel(weight) for weight in weights]
    taps = weights[0].shape[0]
    in_stack = stack_taps(values)
    first = jnp.tanh(apply(flats[0], in_stack))
    first_stack = stack_taps(first)
    second = jnp.tanh(apply(flats[1], first_stack))
    second_stack = stack_taps(second)
    last_grad = jnp.einsum("soml,scml->oc", adjoint, second_stack, precision=highest)
    back = jnp.einsum("oc,soml->scml", flats[2], adjoint, precision=highest)
    second_delta = unstack_taps(back, second.shape[1]) * (1.0 - second * second)
    middle_grad = jnp.einsum("soml,scml->oc", second_delta, first_stack, precision=highest)
    back = jnp.einsum("oc,soml->scml", flats[1], second_delta, precision=highest)
    first_delta = unstack_taps(back, first.shape[1]) * (1.0 - first * first)
    first_grad = jnp.einsum("soml,scml->oc", first_delta, in_stack, precision=highest)
    back = jnp.einsum("oc,soml->scml", flats[0], first_delta, precision=highest)
    input_grad = unstack_taps(back, values.shape[1])
    grads = (kernel_of(first_grad, taps), kernel_of(middle_grad, taps), kernel_of(last_grad, taps))
    return grads, input_grad


LANES = 128


def butterfly_sum(values, axes):
    for axis in axes:
        size = lax.axis_size(axis)
        stride = 1
        while stride < size:
            def partner(offset):
                return lax.ppermute(values, axis, [(i, i ^ offset) for i in range(size)])

            if 4 * stride <= size:
                values = (values + partner(stride)) + (partner(2 * stride) + partner(3 * stride))
                stride *= 4
            else:
                values = values + partner(stride)
                stride *= 2
    return values


def pack(parts):
    flat = jnp.concatenate([part.reshape(-1) for part in parts])
    rows = -(-flat.shape[0] // LANES)
    flat = jnp.pad(flat, (0, rows * LANES - flat.shape[0]))
    return flat.reshape(rows, LANES)


def unpack(total, parts):
    total = total.reshape(-1)
    out, start = [], 0
    for part in parts:
        out.append(total[start : start + part.size].reshape(part.shape))
        start += part.size
    return out


def on_device(
    tracer,
    velocity,
    tracer_adjoint,
    velocity_adjoint,
    sea_mask,
    face_east,
    face_north,
    viscosity,
    conv_first,
    conv_middle,
    conv_last,
):
    levels = tracer.shape[0]
    tile_rows = tracer.shape[1]
    tile_cols = tracer.shape[2]
    sea_cells = sea_mask.astype(jnp.float32)
    planes = jnp.concatenate(
        [tracer_adjoint, velocity_adjoint, sea_cells, face_east[None], face_north[None]], axis=0
    )
    plane_halo = edges(planes)
    weights = (conv_first, conv_middle, conv_last)
    inputs = jnp.concatenate([tracer, velocity], axis=0)
    masked_adjoint = jnp.concatenate(
        [tracer_adjoint * sea_cells, velocity_adjoint * sea_cells], axis=0
    )
    stacked = jnp.concatenate([inputs, masked_adjoint], axis=0)
    blocks = lax.axis_size("lon")
    chunks = stacked.reshape(stacked.shape[0], tile_rows // blocks, blocks, tile_cols)
    band = lax.all_to_all(chunks.transpose(2, 0, 1, 3), "lon", split_axis=0, concat_axis=0, tiled=True)
    weight_grads, band_grad = network_vjp(weights, band[:, : 2 * levels], band[:, 2 * levels :])
    packed = pack(weight_grads)
    packed, plane_halo = lax.optimization_barrier((packed, plane_halo))
    summed = unpack(butterfly_sum(packed, ("lat", "lon")), weight_grads)
    returned = lax.all_to_all(band_grad, "lon", split_axis=0, concat_axis=0, tiled=True)
    input_grad = returned.transpose(1, 2, 0, 3).reshape(2 * levels, tile_rows, tile_cols)
    below, above, left, right = plane_halo
    below = below * row_inside(-1)
    above = above * row_inside(1)

    def part(lo, hi):
        return tuple(piece[lo:hi] for piece in (below, above, left, right))

    sea_near = shifted(sea_cells, part(2 * levels, 3 * levels))
    face_west = jnp.concatenate([left[3 * levels], face_east[:, :-1]], axis=-1)
    face_south = jnp.concatenate([below[3 * levels + 1], face_north[:-1, :]], axis=-2)
    faces = (face_east, face_west, face_north, face_south)
    tracer_term = laplace(tracer_adjoint, part(0, levels), sea_cells, sea_near, *faces)
    first_laplace = laplace(velocity_adjoint, part(levels, 2 * levels), sea_cells, sea_near, *faces)
    scaled = viscosity * first_laplace
    viscous_term = laplace(scaled, edges(scaled), sea_cells, sea_near, *faces)
    scale = 1.0 / math.sqrt(tile_rows * lax.axis_size("lat") * tile_cols * lax.axis_size("lon"))
    tracer_grad = tracer_adjoint + tracer_term + input_grad[:levels]
    velocity_grad = velocity_adjoint - viscous_term + input_grad[levels:]
    return (tracer_grad, velocity_grad, summed[0] * scale, summed[1] * scale, summed[2] * scale)


def solution(mesh):
    return jax.shard_map(
        on_device,
        mesh=mesh,
        in_specs=(
            P(None, "lat", "lon"),
            P(None, "lat", "lon"),
            P(None, "lat", "lon"),
            P(None, "lat", "lon"),
            P(None, "lat", "lon"),
            P("lat", "lon"),
            P("lat", "lon"),
            P("lat", "lon"),
            P(),
            P(),
            P(),
        ),
        out_specs=(P(None, "lat", "lon"), P(None, "lat", "lon"), P(), P(), P()),
        check_vma=False,
    )
```

```python
import math

import jax
import jax.numpy as jnp
from jax import lax
from jax.sharding import PartitionSpec as P

KW = 3


highest = lax.Precision.HIGH


def edges(block):
    def ring(axis, step):
        count = lax.axis_size(axis)
        return [(i, (i + step) % count) for i in range(count)]

    below = lax.ppermute(block[..., -1:, :], "lat", ring("lat", 1))
    above = lax.ppermute(block[..., :1, :], "lat", ring("lat", -1))
    left = lax.ppermute(block[..., :, -1], "lon", ring("lon", 1))
    right = lax.ppermute(block[..., :, 0], "lon", ring("lon", -1))
    return below, above, left, right


def shifted(block, halo):
    below, above, left, right = halo
    east = jnp.concatenate([block[..., :, 1:], right[..., None]], axis=-1)
    west = jnp.concatenate([left[..., None], block[..., :, :-1]], axis=-1)
    north = jnp.concatenate([block[..., 1:, :], above], axis=-2)
    south = jnp.concatenate([below, block[..., :-1, :]], axis=-2)
    return east, west, north, south


def laplace(values, value_halo, sea, sea_near, face_east, face_west, face_north, face_south):
    east, west, north, south = shifted(values, value_halo)
    sea_east, sea_west, sea_north, sea_south = sea_near
    summed = face_east * sea * sea_east * (east - values)
    summed = summed + face_west * sea_west * sea * (west - values)
    summed = summed + face_north * sea * sea_north * (north - values)
    summed = summed + face_south * sea_south * sea * (south - values)
    return summed


def row_inside(step):
    index = lax.axis_index("lat") + step
    return ((index >= 0) & (index < lax.axis_size("lat"))).astype(jnp.float32)


def lon_roll(values, step):
    if step == 1:
        return jnp.concatenate([jnp.roll(values[..., -1:], 1, axis=0), values[..., :-1]], axis=-1)
    if step == -1:
        return jnp.concatenate([values[..., 1:], jnp.roll(values[..., :1], -1, axis=0)], axis=-1)
    return values


def stack_taps(values):
    return jnp.concatenate([lon_roll(values, 1), values, lon_roll(values, -1)], axis=1)


def unstack_taps(stacked, channels):
    first = lon_roll(stacked[:, :channels], -1)
    middle = stacked[:, channels : 2 * channels]
    last = lon_roll(stacked[:, 2 * channels :], 1)
    return first + middle + last


def flat_kernel(kernel):
    taps, outs, ins = kernel.shape
    return kernel.transpose(1, 0, 2).reshape(outs, taps * ins)


def kernel_of(flat, taps):
    outs, width = flat.shape
    return flat.reshape(outs, taps, width // taps).transpose(1, 0, 2)


def apply(flat, stacked):
    return jnp.einsum("oc,scml->soml", flat, stacked, precision=highest)


def network_vjp(weights, values, adjoint):
    flats = [flat_kernel(weight) for weight in weights]
    taps = weights[0].shape[0]
    in_stack = stack_taps(values)
    first = jnp.tanh(apply(flats[0], in_stack))
    first_stack = stack_taps(first)
    second = jnp.tanh(apply(flats[1], first_stack))
    second_stack = stack_taps(second)
    last_grad = jnp.einsum("soml,scml->oc", adjoint, second_stack, precision=highest)
    back = jnp.einsum("oc,soml->scml", flats[2], adjoint, precision=highest)
    second_delta = unstack_taps(back, second.shape[1]) * (1.0 - second * second)
    middle_grad = jnp.einsum("soml,scml->oc", second_delta, first_stack, precision=highest)
    back = jnp.einsum("oc,soml->scml", flats[1], second_delta, precision=highest)
    first_delta = unstack_taps(back, first.shape[1]) * (1.0 - first * first)
    first_grad = jnp.einsum("soml,scml->oc", first_delta, in_stack, precision=highest)
    back = jnp.einsum("oc,soml->scml", flats[0], first_delta, precision=highest)
    input_grad = unstack_taps(back, values.shape[1])
    grads = (kernel_of(first_grad, taps), kernel_of(middle_grad, taps), kernel_of(last_grad, taps))
    return grads, input_grad


LANES = 128


def butterfly_sum(values, axes):
    for axis in axes:
        size = lax.axis_size(axis)
        stride = 1
        while stride < size:
            pairs = [(i, i ^ stride) for i in range(size)]
            values = values + lax.ppermute(values, axis, pairs)
            stride *= 2
    return values


def pack(parts):
    flat = jnp.concatenate([part.reshape(-1) for part in parts])
    rows = -(-flat.shape[0] // LANES)
    flat = jnp.pad(flat, (0, rows * LANES - flat.shape[0]))
    return flat.reshape(rows, LANES)


def unpack(total, parts):
    total = total.reshape(-1)
    out, start = [], 0
    for part in parts:
        out.append(total[start : start + part.size].reshape(part.shape))
        start += part.size
    return out


def on_device(
    tracer,
    velocity,
    tracer_adjoint,
    velocity_adjoint,
    sea_mask,
    face_east,
    face_north,
    viscosity,
    conv_first,
    conv_middle,
    conv_last,
):
    levels = tracer.shape[0]
    tile_rows = tracer.shape[1]
    tile_cols = tracer.shape[2]
    sea_cells = sea_mask.astype(jnp.float32)
    planes = jnp.concatenate(
        [tracer_adjoint, velocity_adjoint, sea_cells, face_east[None], face_north[None]], axis=0
    )
    plane_halo = edges(planes)
    weights = (conv_first, conv_middle, conv_last)
    inputs = jnp.concatenate([tracer, velocity], axis=0)
    masked_adjoint = jnp.concatenate(
        [tracer_adjoint * sea_cells, velocity_adjoint * sea_cells], axis=0
    )
    stacked = jnp.concatenate([inputs, masked_adjoint], axis=0)
    blocks = lax.axis_size("lon")
    chunks = stacked.reshape(stacked.shape[0], tile_rows // blocks, blocks, tile_cols)
    band = lax.all_to_all(chunks.transpose(2, 0, 1, 3), "lon", split_axis=0, concat_axis=0, tiled=True)
    weight_grads, band_grad = network_vjp(weights, band[:, : 2 * levels], band[:, 2 * levels :])
    packed = pack(weight_grads)
    packed, plane_halo = lax.optimization_barrier((packed, plane_halo))
    summed = unpack(butterfly_sum(packed, ("lon", "lat")), weight_grads)
    returned = lax.all_to_all(band_grad, "lon", split_axis=0, concat_axis=0, tiled=True)
    input_grad = returned.transpose(1, 2, 0, 3).reshape(2 * levels, tile_rows, tile_cols)
    below, above, left, right = plane_halo
    below = below * row_inside(-1)
    above = above * row_inside(1)

    def part(lo, hi):
        return tuple(piece[lo:hi] for piece in (below, above, left, right))

    sea_near = shifted(sea_cells, part(2 * levels, 3 * levels))
    face_west = jnp.concatenate([left[3 * levels][:, None], face_east[:, :-1]], axis=-1)
    face_south = jnp.concatenate([below[3 * levels + 1], face_north[:-1, :]], axis=-2)
    faces = (face_east, face_west, face_north, face_south)
    tracer_term = laplace(tracer_adjoint, part(0, levels), sea_cells, sea_near, *faces)
    first_laplace = laplace(velocity_adjoint, part(levels, 2 * levels), sea_cells, sea_near, *faces)
    scaled = viscosity * first_laplace
    viscous_term = laplace(scaled, edges(scaled), sea_cells, sea_near, *faces)
    scale = 1.0 / math.sqrt(tile_rows * lax.axis_size("lat") * tile_cols * lax.axis_size("lon"))
    tracer_grad = tracer_adjoint + tracer_term + input_grad[:levels]
    velocity_grad = velocity_adjoint - viscous_term + input_grad[levels:]
    return (tracer_grad, velocity_grad, summed[0] * scale, summed[1] * scale, summed[2] * scale)


def solution(mesh):
    return jax.shard_map(
        on_device,
        mesh=mesh,
        in_specs=(
            P(None, "lat", "lon"),
            P(None, "lat", "lon"),
            P(None, "lat", "lon"),
            P(None, "lat", "lon"),
            P(None, "lat", "lon"),
            P("lat", "lon"),
            P("lat", "lon"),
            P("lat", "lon"),
            P(),
            P(),
            P(),
        ),
        out_specs=(P(None, "lat", "lon"), P(None, "lat", "lon"), P(), P(), P()),
        check_vma=False,
    )
```

```python
import math

import jax
import jax.numpy as jnp
from jax import lax
from jax.sharding import PartitionSpec as P

KW = 3


highest = lax.Precision.HIGH


def edges(block):
    def ring(axis, step):
        count = lax.axis_size(axis)
        return [(i, (i + step) % count) for i in range(count)]

    below = lax.ppermute(block[..., -1:, :], "lat", ring("lat", 1))
    above = lax.ppermute(block[..., :1, :], "lat", ring("lat", -1))
    left = lax.ppermute(block[..., :, -1:], "lon", ring("lon", 1))
    right = lax.ppermute(block[..., :, :1], "lon", ring("lon", -1))
    return below, above, left, right


def shifted(block, halo):
    below, above, left, right = halo
    east = jnp.concatenate([block[..., :, 1:], right], axis=-1)
    west = jnp.concatenate([left, block[..., :, :-1]], axis=-1)
    north = jnp.concatenate([block[..., 1:, :], above], axis=-2)
    south = jnp.concatenate([below, block[..., :-1, :]], axis=-2)
    return east, west, north, south


def laplace(values, value_halo, sea, sea_near, face_east, face_west, face_north, face_south):
    east, west, north, south = shifted(values, value_halo)
    sea_east, sea_west, sea_north, sea_south = sea_near
    summed = face_east * sea * sea_east * (east - values)
    summed = summed + face_west * sea_west * sea * (west - values)
    summed = summed + face_north * sea * sea_north * (north - values)
    summed = summed + face_south * sea_south * sea * (south - values)
    return summed


def row_inside(step):
    index = lax.axis_index("lat") + step
    return ((index >= 0) & (index < lax.axis_size("lat"))).astype(jnp.float32)


def lon_roll(values, step):
    if step == 1:
        return jnp.concatenate([jnp.roll(values[..., -1:], 1, axis=0), values[..., :-1]], axis=-1)
    if step == -1:
        return jnp.concatenate([values[..., 1:], jnp.roll(values[..., :1], -1, axis=0)], axis=-1)
    return values


def stack_taps(values):
    return jnp.concatenate([lon_roll(values, 1), values, lon_roll(values, -1)], axis=1)


def unstack_taps(stacked, channels):
    first = lon_roll(stacked[:, :channels], -1)
    middle = stacked[:, channels : 2 * channels]
    last = lon_roll(stacked[:, 2 * channels :], 1)
    return first + middle + last


def flat_kernel(kernel):
    taps, outs, ins = kernel.shape
    return kernel.transpose(1, 0, 2).reshape(outs, taps * ins)


def kernel_of(flat, taps):
    outs, width = flat.shape
    return flat.reshape(outs, taps, width // taps).transpose(1, 0, 2)


def apply(flat, stacked):
    return jnp.einsum("oc,scml->soml", flat, stacked, precision=highest)


def network_vjp(weights, values, adjoint):
    flats = [flat_kernel(weight) for weight in weights]
    taps = weights[0].shape[0]
    in_stack = stack_taps(values)
    first = jnp.tanh(apply(flats[0], in_stack))
    first_stack = stack_taps(first)
    second = jnp.tanh(apply(flats[1], first_stack))
    second_stack = stack_taps(second)
    last_grad = jnp.einsum("soml,scml->oc", adjoint, second_stack, precision=highest)
    back = jnp.einsum("oc,soml->scml", flats[2], adjoint, precision=highest)
    second_delta = unstack_taps(back, second.shape[1]) * (1.0 - second * second)
    middle_grad = jnp.einsum("soml,scml->oc", second_delta, first_stack, precision=highest)
    back = jnp.einsum("oc,soml->scml", flats[1], second_delta, precision=highest)
    first_delta = unstack_taps(back, first.shape[1]) * (1.0 - first * first)
    first_grad = jnp.einsum("soml,scml->oc", first_delta, in_stack, precision=highest)
    grads = (kernel_of(first_grad, taps), kernel_of(middle_grad, taps), kernel_of(last_grad, taps))
    return grads, first_delta


def input_pullback(weights, first_delta, channels):
    back = jnp.einsum("oc,soml->scml", flat_kernel(weights[0]), first_delta, precision=highest)
    return unstack_taps(back, channels)


LANES = 128


def butterfly_sum(values, axes, tie):
    first = True
    for axis in axes:
        size = lax.axis_size(axis)
        stride = 1
        while stride < size:
            pairs = [(i, i ^ stride) for i in range(size)]
            values = values + lax.ppermute(values, axis, pairs)
            if first:
                values, tie = lax.optimization_barrier((values, tie))
                first = False
            stride *= 2
    return values, tie


def pack(parts):
    flat = jnp.concatenate([part.reshape(-1) for part in parts])
    rows = -(-flat.shape[0] // LANES)
    flat = jnp.pad(flat, (0, rows * LANES - flat.shape[0]))
    return flat.reshape(rows, LANES)


def unpack(total, parts):
    total = total.reshape(-1)
    out, start = [], 0
    for part in parts:
        out.append(total[start : start + part.size].reshape(part.shape))
        start += part.size
    return out


def on_device(
    tracer,
    velocity,
    tracer_adjoint,
    velocity_adjoint,
    sea_mask,
    face_east,
    face_north,
    viscosity,
    conv_first,
    conv_middle,
    conv_last,
):
    levels = tracer.shape[0]
    tile_rows = tracer.shape[1]
    tile_cols = tracer.shape[2]
    sea_cells = sea_mask.astype(jnp.float32)
    planes = jnp.concatenate(
        [tracer_adjoint, velocity_adjoint, sea_cells, face_east[None], face_north[None]], axis=0
    )
    plane_halo = edges(planes)
    weights = (conv_first, conv_middle, conv_last)
    inputs = jnp.concatenate([tracer, velocity], axis=0)
    masked_adjoint = jnp.concatenate(
        [tracer_adjoint * sea_cells, velocity_adjoint * sea_cells], axis=0
    )
    stacked = jnp.concatenate([inputs, masked_adjoint], axis=0)
    blocks = lax.axis_size("lon")
    chunks = stacked.reshape(stacked.shape[0], tile_rows // blocks, blocks, tile_cols)
    band = lax.all_to_all(chunks.transpose(2, 0, 1, 3), "lon", split_axis=0, concat_axis=0, tiled=True)
    weight_grads, first_delta = network_vjp(weights, band[:, : 2 * levels], band[:, 2 * levels :])
    packed = pack(weight_grads)
    packed, plane_halo = lax.optimization_barrier((packed, plane_halo))
    total, first_delta = butterfly_sum(packed, ("lon", "lat"), first_delta)
    summed = unpack(total, weight_grads)
    band_grad = input_pullback(weights, first_delta, 2 * levels)
    returned = lax.all_to_all(band_grad, "lon", split_axis=0, concat_axis=0, tiled=True)
    input_grad = returned.transpose(1, 2, 0, 3).reshape(2 * levels, tile_rows, tile_cols)
    below, above, left, right = plane_halo
    below = below * row_inside(-1)
    above = above * row_inside(1)

    def part(lo, hi):
        return tuple(piece[lo:hi] for piece in (below, above, left, right))

    sea_near = shifted(sea_cells, part(2 * levels, 3 * levels))
    face_west = jnp.concatenate([left[3 * levels], face_east[:, :-1]], axis=-1)
    face_south = jnp.concatenate([below[3 * levels + 1], face_north[:-1, :]], axis=-2)
    faces = (face_east, face_west, face_north, face_south)
    tracer_term = laplace(tracer_adjoint, part(0, levels), sea_cells, sea_near, *faces)
    first_laplace = laplace(velocity_adjoint, part(levels, 2 * levels), sea_cells, sea_near, *faces)
    scaled = viscosity * first_laplace
    viscous_term = laplace(scaled, edges(scaled), sea_cells, sea_near, *faces)
    scale = 1.0 / math.sqrt(tile_rows * lax.axis_size("lat") * tile_cols * lax.axis_size("lon"))
    tracer_grad = tracer_adjoint + tracer_term + input_grad[:levels]
    velocity_grad = velocity_adjoint - viscous_term + input_grad[levels:]
    return (tracer_grad, velocity_grad, summed[0] * scale, summed[1] * scale, summed[2] * scale)


def solution(mesh):
    return jax.shard_map(
        on_device,
        mesh=mesh,
        in_specs=(
            P(None, "lat", "lon"),
            P(None, "lat", "lon"),
            P(None, "lat", "lon"),
            P(None, "lat", "lon"),
            P(None, "lat", "lon"),
            P("lat", "lon"),
            P("lat", "lon"),
            P("lat", "lon"),
            P(),
            P(),
            P(),
        ),
        out_specs=(P(None, "lat", "lon"), P(None, "lat", "lon"), P(), P(), P()),
        check_vma=False,
    )
```

```python
import math

import jax
import jax.numpy as jnp
from jax import lax
from jax.sharding import PartitionSpec as P

KW = 3


highest = lax.Precision.HIGH


def edges(block):
    def ring(axis, step):
        count = lax.axis_size(axis)
        return [(i, (i + step) % count) for i in range(count)]

    below = lax.ppermute(block[..., -1:, :], "lat", ring("lat", 1))
    above = lax.ppermute(block[..., :1, :], "lat", ring("lat", -1))
    left = lax.ppermute(block[..., :, -1:], "lon", ring("lon", 1))
    right = lax.ppermute(block[..., :, :1], "lon", ring("lon", -1))
    return below, above, left, right


def shifted(block, halo):
    below, above, left, right = halo
    east = jnp.concatenate([block[..., :, 1:], right], axis=-1)
    west = jnp.concatenate([left, block[..., :, :-1]], axis=-1)
    north = jnp.concatenate([block[..., 1:, :], above], axis=-2)
    south = jnp.concatenate([below, block[..., :-1, :]], axis=-2)
    return east, west, north, south


def laplace(values, value_halo, sea, sea_near, face_east, face_west, face_north, face_south):
    east, west, north, south = shifted(values, value_halo)
    sea_east, sea_west, sea_north, sea_south = sea_near
    summed = face_east * sea * sea_east * (east - values)
    summed = summed + face_west * sea_west * sea * (west - values)
    summed = summed + face_north * sea * sea_north * (north - values)
    summed = summed + face_south * sea_south * sea * (south - values)
    return summed


def row_inside(step):
    index = lax.axis_index("lat") + step
    return ((index >= 0) & (index < lax.axis_size("lat"))).astype(jnp.float32)


def lon_roll(values, step):
    if step == 1:
        return jnp.concatenate([jnp.roll(values[..., -1:], 1, axis=0), values[..., :-1]], axis=-1)
    if step == -1:
        return jnp.concatenate([values[..., 1:], jnp.roll(values[..., :1], -1, axis=0)], axis=-1)
    return values


def stack_taps(values):
    return jnp.concatenate([lon_roll(values, 1), values, lon_roll(values, -1)], axis=1)


def unstack_taps(stacked, channels):
    first = lon_roll(stacked[:, :channels], -1)
    middle = stacked[:, channels : 2 * channels]
    last = lon_roll(stacked[:, 2 * channels :], 1)
    return first + middle + last


def flat_kernel(kernel):
    taps, outs, ins = kernel.shape
    return kernel.transpose(1, 0, 2).reshape(outs, taps * ins)


def kernel_of(flat, taps):
    outs, width = flat.shape
    return flat.reshape(outs, taps, width // taps).transpose(1, 0, 2)


def apply(flat, stacked):
    return jnp.einsum("oc,scml->soml", flat, stacked, precision=highest)


def network_vjp(weights, values, adjoint):
    flats = [flat_kernel(weight) for weight in weights]
    taps = weights[0].shape[0]
    in_stack = stack_taps(values)
    first = jnp.tanh(apply(flats[0], in_stack))
    first_stack = stack_taps(first)
    second = jnp.tanh(apply(flats[1], first_stack))
    second_stack = stack_taps(second)
    last_grad = jnp.einsum("soml,scml->oc", adjoint, second_stack, precision=highest)
    back = jnp.einsum("oc,soml->scml", flats[2], adjoint, precision=highest)
    second_delta = unstack_taps(back, second.shape[1]) * (1.0 - second * second)
    middle_grad = jnp.einsum("soml,scml->oc", second_delta, first_stack, precision=highest)
    back = jnp.einsum("oc,soml->scml", flats[1], second_delta, precision=highest)
    first_delta = unstack_taps(back, first.shape[1]) * (1.0 - first * first)
    first_grad = jnp.einsum("soml,scml->oc", first_delta, in_stack, precision=highest)
    grads = (kernel_of(first_grad, taps), kernel_of(middle_grad, taps), kernel_of(last_grad, taps))
    return grads, first_delta


def input_pullback(weights, first_delta, channels):
    back = jnp.einsum("oc,soml->scml", flat_kernel(weights[0]), first_delta, precision=highest)
    return unstack_taps(back, channels)


LANES = 128


def butterfly_sum(values, axes, tie, late):
    rounds = []
    for axis in axes:
        stride = 1
        while stride < lax.axis_size(axis):
            rounds.append((axis, stride))
            stride *= 2
    for index, (axis, stride) in enumerate(rounds):
        if index == len(rounds) - 1:
            values, late = lax.optimization_barrier((values, late))
        pairs = [(i, i ^ stride) for i in range(lax.axis_size(axis))]
        values = values + lax.ppermute(values, axis, pairs)
        if index == 0:
            values, tie = lax.optimization_barrier((values, tie))
    return values, tie, late


def pack(parts):
    flat = jnp.concatenate([part.reshape(-1) for part in parts])
    rows = -(-flat.shape[0] // LANES)
    flat = jnp.pad(flat, (0, rows * LANES - flat.shape[0]))
    return flat.reshape(rows, LANES)


def unpack(total, parts):
    total = total.reshape(-1)
    out, start = [], 0
    for part in parts:
        out.append(total[start : start + part.size].reshape(part.shape))
        start += part.size
    return out


def on_device(
    tracer,
    velocity,
    tracer_adjoint,
    velocity_adjoint,
    sea_mask,
    face_east,
    face_north,
    viscosity,
    conv_first,
    conv_middle,
    conv_last,
):
    levels = tracer.shape[0]
    tile_rows = tracer.shape[1]
    tile_cols = tracer.shape[2]
    sea_cells = sea_mask.astype(jnp.float32)
    planes = jnp.concatenate(
        [tracer_adjoint, velocity_adjoint, sea_cells, face_east[None], face_north[None]], axis=0
    )
    plane_halo = edges(planes)
    weights = (conv_first, conv_middle, conv_last)
    inputs = jnp.concatenate([tracer, velocity], axis=0)
    masked_adjoint = jnp.concatenate(
        [tracer_adjoint * sea_cells, velocity_adjoint * sea_cells], axis=0
    )
    stacked = jnp.concatenate([inputs, masked_adjoint], axis=0)
    blocks = lax.axis_size("lon")
    chunks = stacked.reshape(stacked.shape[0], tile_rows // blocks, blocks, tile_cols)
    band = lax.all_to_all(chunks.transpose(2, 0, 1, 3), "lon", split_axis=0, concat_axis=0, tiled=True)
    weight_grads, first_delta = network_vjp(weights, band[:, : 2 * levels], band[:, 2 * levels :])
    packed = pack(weight_grads)
    packed, plane_halo = lax.optimization_barrier((packed, plane_halo))

    below, above, left, right = plane_halo
    below = below * row_inside(-1)
    above = above * row_inside(1)

    def part(lo, hi):
        return tuple(piece[lo:hi] for piece in (below, above, left, right))

    sea_near = shifted(sea_cells, part(2 * levels, 3 * levels))
    face_west = jnp.concatenate([left[3 * levels], face_east[:, :-1]], axis=-1)
    face_south = jnp.concatenate([below[3 * levels + 1], face_north[:-1, :]], axis=-2)
    faces = (face_east, face_west, face_north, face_south)
    tracer_term = laplace(tracer_adjoint, part(0, levels), sea_cells, sea_near, *faces)
    first_laplace = laplace(velocity_adjoint, part(levels, 2 * levels), sea_cells, sea_near, *faces)
    scaled = viscosity * first_laplace
    total, first_delta, scaled_halo = butterfly_sum(packed, ("lon", "lat"), first_delta, edges(scaled))
    summed = unpack(total, weight_grads)
    band_grad = input_pullback(weights, first_delta, 2 * levels)
    returned = lax.all_to_all(band_grad, "lon", split_axis=0, concat_axis=0, tiled=True)
    input_grad = returned.transpose(1, 2, 0, 3).reshape(2 * levels, tile_rows, tile_cols)
    viscous_term = laplace(scaled, scaled_halo, sea_cells, sea_near, *faces)
    scale = 1.0 / math.sqrt(tile_rows * lax.axis_size("lat") * tile_cols * lax.axis_size("lon"))
    tracer_grad = tracer_adjoint + tracer_term + input_grad[:levels]
    velocity_grad = velocity_adjoint - viscous_term + input_grad[levels:]
    return (tracer_grad, velocity_grad, summed[0] * scale, summed[1] * scale, summed[2] * scale)


def solution(mesh):
    return jax.shard_map(
        on_device,
        mesh=mesh,
        in_specs=(
            P(None, "lat", "lon"),
            P(None, "lat", "lon"),
            P(None, "lat", "lon"),
            P(None, "lat", "lon"),
            P(None, "lat", "lon"),
            P("lat", "lon"),
            P("lat", "lon"),
            P("lat", "lon"),
            P(),
            P(),
            P(),
        ),
        out_specs=(P(None, "lat", "lon"), P(None, "lat", "lon"), P(), P(), P()),
        check_vma=False,
    )
```

```python
import math

import jax
import jax.numpy as jnp
from jax import lax
from jax.sharding import PartitionSpec as P

KW = 3


highest = lax.Precision.HIGH


def edges(block):
    def ring(axis, step):
        count = lax.axis_size(axis)
        return [(i, (i + step) % count) for i in range(count)]

    below = lax.ppermute(block[..., -1:, :], "lat", ring("lat", 1))
    above = lax.ppermute(block[..., :1, :], "lat", ring("lat", -1))
    left = lax.ppermute(block[..., :, -1:], "lon", ring("lon", 1))
    right = lax.ppermute(block[..., :, :1], "lon", ring("lon", -1))
    return below, above, left, right


def shifted(block, halo):
    below, above, left, right = halo
    east = jnp.concatenate([block[..., :, 1:], right], axis=-1)
    west = jnp.concatenate([left, block[..., :, :-1]], axis=-1)
    north = jnp.concatenate([block[..., 1:, :], above], axis=-2)
    south = jnp.concatenate([below, block[..., :-1, :]], axis=-2)
    return east, west, north, south


def laplace(values, value_halo, sea, sea_near, face_east, face_west, face_north, face_south):
    east, west, north, south = shifted(values, value_halo)
    sea_east, sea_west, sea_north, sea_south = sea_near
    summed = face_east * sea * sea_east * (east - values)
    summed = summed + face_west * sea_west * sea * (west - values)
    summed = summed + face_north * sea * sea_north * (north - values)
    summed = summed + face_south * sea_south * sea * (south - values)
    return summed


def row_inside(step):
    index = lax.axis_index("lat") + step
    return ((index >= 0) & (index < lax.axis_size("lat"))).astype(jnp.float32)


def lon_roll(values, step):
    if step == 1:
        return jnp.concatenate([jnp.roll(values[..., -1:], 1, axis=0), values[..., :-1]], axis=-1)
    if step == -1:
        return jnp.concatenate([values[..., 1:], jnp.roll(values[..., :1], -1, axis=0)], axis=-1)
    return values


def stack_taps(values):
    return jnp.concatenate([lon_roll(values, 1), values, lon_roll(values, -1)], axis=1)


def unstack_taps(stacked, channels):
    first = lon_roll(stacked[:, :channels], -1)
    middle = stacked[:, channels : 2 * channels]
    last = lon_roll(stacked[:, 2 * channels :], 1)
    return first + middle + last


def flat_kernel(kernel):
    taps, outs, ins = kernel.shape
    return kernel.transpose(1, 0, 2).reshape(outs, taps * ins)


def kernel_of(flat, taps):
    outs, width = flat.shape
    return flat.reshape(outs, taps, width // taps).transpose(1, 0, 2)


def apply(flat, stacked):
    return jnp.einsum("oc,scml->soml", flat, stacked, precision=highest)


def network_vjp(weights, values, adjoint):
    flats = [flat_kernel(weight) for weight in weights]
    taps = weights[0].shape[0]
    in_stack = stack_taps(values)
    first = jnp.tanh(apply(flats[0], in_stack))
    first_stack = stack_taps(first)
    second = jnp.tanh(apply(flats[1], first_stack))
    second_stack = stack_taps(second)
    last_grad = jnp.einsum("soml,scml->oc", adjoint, second_stack, precision=highest)
    back = jnp.einsum("oc,soml->scml", flats[2], adjoint, precision=highest)
    second_delta = unstack_taps(back, second.shape[1]) * (1.0 - second * second)
    middle_grad = jnp.einsum("soml,scml->oc", second_delta, first_stack, precision=highest)
    back = jnp.einsum("oc,soml->scml", flats[1], second_delta, precision=highest)
    first_delta = unstack_taps(back, first.shape[1]) * (1.0 - first * first)
    first_grad = jnp.einsum("soml,scml->oc", first_delta, in_stack, precision=highest)
    grads = (kernel_of(first_grad, taps), kernel_of(middle_grad, taps), kernel_of(last_grad, taps))
    return grads, first_delta


def input_pullback(weights, first_delta, channels):
    back = jnp.einsum("oc,soml->scml", flat_kernel(weights[0]), first_delta, precision=highest)
    return unstack_taps(back, channels)


LANES = 128


def butterfly_sum(values, axes, tie):
    first = True
    for axis in axes:
        size = lax.axis_size(axis)
        stride = 1
        while stride < size:
            pairs = [(i, i ^ stride) for i in range(size)]
            values = values + lax.ppermute(values, axis, pairs)
            if first:
                values, tie = lax.optimization_barrier((values, tie))
                first = False
            stride *= 2
    return values, tie


def pack(parts):
    flat = jnp.concatenate([part.reshape(-1) for part in parts])
    rows = -(-flat.shape[0] // LANES)
    flat = jnp.pad(flat, (0, rows * LANES - flat.shape[0]))
    return flat.reshape(rows, LANES)


def unpack(total, parts):
    total = total.reshape(-1)
    out, start = [], 0
    for part in parts:
        out.append(total[start : start + part.size].reshape(part.shape))
        start += part.size
    return out


def on_device(
    tracer,
    velocity,
    tracer_adjoint,
    velocity_adjoint,
    sea_mask,
    face_east,
    face_north,
    viscosity,
    conv_first,
    conv_middle,
    conv_last,
):
    levels = tracer.shape[0]
    tile_rows = tracer.shape[1]
    tile_cols = tracer.shape[2]
    sea_cells = sea_mask.astype(jnp.float32)
    planes = jnp.concatenate(
        [tracer_adjoint, velocity_adjoint, sea_cells, face_east[None], face_north[None]], axis=0
    )
    plane_halo = edges(planes)
    weights = (conv_first, conv_middle, conv_last)
    inputs = jnp.concatenate([tracer, velocity], axis=0)
    masked_adjoint = jnp.concatenate(
        [tracer_adjoint * sea_cells, velocity_adjoint * sea_cells], axis=0
    )
    stacked = jnp.concatenate([inputs, masked_adjoint], axis=0)
    blocks = lax.axis_size("lon")
    chunks = stacked.reshape(stacked.shape[0], tile_rows // blocks, blocks, tile_cols)
    band = lax.all_to_all(chunks.transpose(2, 0, 1, 3), "lon", split_axis=0, concat_axis=0, tiled=True)
    weight_grads, first_delta = network_vjp(weights, band[:, : 2 * levels], band[:, 2 * levels :])
    packed = pack(weight_grads)
    packed, plane_halo = lax.optimization_barrier((packed, plane_halo))
    total, first_delta = butterfly_sum(packed, ("lat", "lon"), first_delta)
    summed = unpack(total, weight_grads)
    band_grad = input_pullback(weights, first_delta, 2 * levels)
    returned = lax.all_to_all(band_grad, "lon", split_axis=0, concat_axis=0, tiled=True)
    input_grad = returned.transpose(1, 2, 0, 3).reshape(2 * levels, tile_rows, tile_cols)
    below, above, left, right = plane_halo
    below = below * row_inside(-1)
    above = above * row_inside(1)

    def part(lo, hi):
        return tuple(piece[lo:hi] for piece in (below, above, left, right))

    sea_near = shifted(sea_cells, part(2 * levels, 3 * levels))
    face_west = jnp.concatenate([left[3 * levels], face_east[:, :-1]], axis=-1)
    face_south = jnp.concatenate([below[3 * levels + 1], face_north[:-1, :]], axis=-2)
    faces = (face_east, face_west, face_north, face_south)
    tracer_term = laplace(tracer_adjoint, part(0, levels), sea_cells, sea_near, *faces)
    first_laplace = laplace(velocity_adjoint, part(levels, 2 * levels), sea_cells, sea_near, *faces)
    scaled = viscosity * first_laplace
    viscous_term = laplace(scaled, edges(scaled), sea_cells, sea_near, *faces)
    scale = 1.0 / math.sqrt(tile_rows * lax.axis_size("lat") * tile_cols * lax.axis_size("lon"))
    tracer_grad = tracer_adjoint + tracer_term + input_grad[:levels]
    velocity_grad = velocity_adjoint - viscous_term + input_grad[levels:]
    return (tracer_grad, velocity_grad, summed[0] * scale, summed[1] * scale, summed[2] * scale)


def solution(mesh):
    return jax.shard_map(
        on_device,
        mesh=mesh,
        in_specs=(
            P(None, "lat", "lon"),
            P(None, "lat", "lon"),
            P(None, "lat", "lon"),
            P(None, "lat", "lon"),
            P(None, "lat", "lon"),
            P("lat", "lon"),
            P("lat", "lon"),
            P("lat", "lon"),
            P(),
            P(),
            P(),
        ),
        out_specs=(P(None, "lat", "lon"), P(None, "lat", "lon"), P(), P(), P()),
        check_vma=False,
    )
```
